256 devices in a mesh: seq: 32 (over x, y, core), tp: 8 (over z).
Axes of the slice: x: 4, y: 4, z: 8, core: 2. Of those that a mesh axis runs over, the one named last changes fastest.
Arguments:
- tokens: bfloat16 [32, 4, 2048], P('seq'), may hold values from -6 to 6
- w_query: bfloat16 [2048, 2048], P(None, 'tp'), may hold values from -0.125 to 0.125
- w_keyval: bfloat16 [2048, 512], replicated, may hold values from -0.3125 to 0.3125
- w_out: bfloat16 [2048, 2048], P('tp'), may hold values from -0.125 to 0.125
- kv_cache: bfloat16 [4608, 8, 128, 128], P('seq', 'tp'), as said below
- lengths: int32 [32], replicated, may hold values from 2048 to 16380, as said below
- page_frame: int32 [32, 128], replicated, may hold values from 0 to 4607, as said below
- dest_frame: int32 [32, 128], replicated, may hold values from 0 to 4607, as said below
Outputs:
- hidden: bfloat16 [32, 4, 2048], P('seq', None, 'tp')
- new_cache: bfloat16 [4608, 8, 128, 128], P('seq', 'tp')
The draws below stay inside these ranges and needn't reach their ends.
Inputs may be any that keep to these rules, and one draw needn't show every extreme that they name: `lengths`: some request holds exactly 16380, some exactly 2048. `page_frame`: frame f lies on seq device f // 144; no two pages share a frame; each seq device holds exactly 128 pages. `dest_frame`: equal to page_frame except for exactly 16 pages leaving each seq device, each into a frame that held no page before; a seq device sends at most one page to each other seq device and receives exactly 16 pages. `kv_cache`: copy c of a frame holds KV head c * 4 // 8, copies of the same head are equal; a slot's first 64 entries are the key, the rest the value.
All inputs are finite; a program needn't handle non-finite values.
Results may differ from the reference program's by a relative error of at most 0.012.
The reference program's roundings to bfloat16 on the way count: a program that leaves them out, or rounds other values in their place, can miss the bound.
Values may be sent and summed in bfloat16 or wider, within the bound.
No kernel may reach another device: no remote copies, remote signals or barrier semaphores. Data moves between devices by JAX's collectives and lax.ppermute only.
A program may use at most 64 MiB of HBM per device.

```python
import jax
import jax.numpy as jnp
from jax import lax

D = 2048
HEADS = 32
KV_HEADS = 4
HEAD = 64
WINDOW = 2048
SLOTS = 128
CONTEXT = 16384
TOK = 4
REQ_DEV = 1
PAGES = 128
REQ = 32
MOVES = 16
PG_DEV = 144
FRAMES = 4608
COPIES = 8


def layout(key):
    sub_keys = [jax.random.fold_in(key, 100 + offset) for offset in range(10)]
    seq_devices = FRAMES // PG_DEV
    hot_count = max(1, seq_devices // 8)
    held_pages = REQ_DEV * PAGES
    total_pages = REQ * PAGES
    move_count = MOVES
    hot_live = 3 * REQ_DEV * (WINDOW // SLOTS)
    req_order = jax.random.permutation(sub_keys[0], REQ)
    req_rank = jnp.argsort(req_order)
    base_len = jax.random.randint(sub_keys[1], (REQ,), WINDOW, CONTEXT - TOK + 1, dtype=jnp.int32)
    lengths = jnp.where(req_rank == 0, CONTEXT - TOK, base_len)
    lengths = jnp.where(req_rank == 1, WINDOW, lengths).astype(jnp.int32)
    page_starts = jnp.arange(PAGES, dtype=jnp.int32)[None, :] * SLOTS
    live_flags = ((page_starts < lengths[:, None]) & (page_starts + SLOTS > lengths[:, None] - WINDOW + 1)).reshape(-1)
    local_key = jax.random.randint(sub_keys[3], (seq_devices, PG_DEV), 0, 1 << 20, dtype=jnp.int32)
    local_order = jnp.argsort(local_key * PG_DEV + jnp.arange(PG_DEV, dtype=jnp.int32)[None, :], axis=1).astype(jnp.int32)
    device_ids = jnp.arange(seq_devices, dtype=jnp.int32)
    held_frames = device_ids[:, None] * PG_DEV + local_order[:, :held_pages]
    hot_start = jax.random.randint(sub_keys[4], (), 0, seq_devices, dtype=jnp.int32)
    is_hot = (device_ids - hot_start) % seq_devices < hot_count
    first_class = is_hot[:, None] & (jnp.arange(held_pages, dtype=jnp.int32)[None, :] < hot_live)
    frame_key = jnp.where(first_class, 0, 1) * (seq_devices * held_pages) + jax.random.permutation(sub_keys[5], seq_devices * held_pages).reshape(seq_devices, held_pages)
    frame_list = held_frames.reshape(-1)[jnp.argsort(frame_key.reshape(-1))]
    page_key = jnp.where(live_flags, 0, 1) * total_pages + jax.random.permutation(sub_keys[6], total_pages)
    page_list = jnp.argsort(page_key)
    old_frame = jnp.zeros((total_pages,), jnp.int32).at[page_list].set(frame_list.astype(jnp.int32))
    extra_offsets = 2 + jax.random.permutation(sub_keys[7], seq_devices - 3)[:move_count - 2]
    offsets = jnp.concatenate([jnp.array([1, seq_devices - 1], jnp.int32), extra_offsets.astype(jnp.int32)])
    pick_key = jax.random.randint(sub_keys[8], (seq_devices, held_pages), 0, 1 << 20, dtype=jnp.int32)
    picked = jnp.argsort(pick_key * held_pages + jnp.arange(held_pages, dtype=jnp.int32)[None, :], axis=1)[:, :move_count]
    source_frame = device_ids[:, None] * PG_DEV + jnp.take_along_axis(local_order[:, :held_pages], picked, axis=1)
    target_device = (device_ids[:, None] + offsets[None, :]) % seq_devices
    free_key = jax.random.randint(sub_keys[9], (seq_devices, move_count), 0, 1 << 20, dtype=jnp.int32)
    free_order = jnp.argsort(free_key * move_count + jnp.arange(move_count, dtype=jnp.int32)[None, :], axis=1)
    free_frames = jnp.take_along_axis(local_order[:, held_pages:], free_order, axis=1)
    column_ids = jnp.broadcast_to(jnp.arange(move_count, dtype=jnp.int32)[None, :], target_device.shape)
    target_frame = target_device * PG_DEV + free_frames[target_device, column_ids]
    inverse = jnp.zeros((seq_devices * PG_DEV,), jnp.int32).at[old_frame].set(jnp.arange(total_pages, dtype=jnp.int32))
    moved_pages = inverse[source_frame.reshape(-1)]
    new_frame = old_frame.at[moved_pages].set(target_frame.reshape(-1).astype(jnp.int32))
    return (lengths, old_frame.reshape(REQ, PAGES), new_frame.reshape(REQ, PAGES))


def draw_lengths(key, part):
    return layout(key)[0]


def draw_page_frame(key, part):
    return layout(key)[1]


def draw_dest_frame(key, part):
    return layout(key)[2]


def draw_kv_cache(key, part):
    sub_keys = [jax.random.fold_in(key, 200 + offset) for offset in range(6)]
    full_shape = (FRAMES, KV_HEADS, SLOTS, 2 * HEAD)
    base_val = jnp.clip(jax.random.normal(sub_keys[0], full_shape, jnp.float32), -6.0, 6.0)
    column_ids = jnp.arange(2 * HEAD)
    entries = base_val * jnp.where(column_ids < HEAD, 2.0, 3.0)
    copies = jnp.repeat(entries, COPIES // KV_HEADS, axis=1)
    return copies.astype(jnp.bfloat16)


def levels(own_key, shape, split, least, largest):
    def one(axis_at, shards_of):
        steps = jax.random.uniform(jax.random.fold_in(jax.random.fold_in(own_key, 6), axis_at), (shards_of,), jnp.float32, least / len(split), largest / len(split))
        return jnp.repeat(jnp.exp(steps), shape[axis_at] // shards_of).reshape((-1,) + (1,) * (len(shape) - axis_at - 1))

    factor_of = one(*split[0])
    for cut in split[1:]:
        factor_of = factor_of * one(*cut)
    return factor_of


def noise(key, dims, width, bound, shards=(), kind=jnp.bfloat16):
    gain = levels(key, dims, shards, -0.22, 0.18) if shards else 1.0
    result = jax.random.normal(key, dims, jnp.float32) * width * gain
    return jnp.minimum(jnp.maximum(result, -bound), bound).astype(kind)


def setup_inputs(seed: int = 0) -> dict:
    seeds = jax.random.split(jax.random.key(seed), 9)
    return {
        "tokens": noise(seeds[0], (REQ, TOK, D), 1.0, 6.0, ((0, 32),)),
        "w_query": noise(seeds[1], (D, HEADS * HEAD), D ** -0.5, 0.125, ((1, 8),)),
        "w_keyval": noise(seeds[2], (D, KV_HEADS * 2 * HEAD), (D // 6) ** -0.5, 0.3125),
        "w_out": noise(seeds[3], (HEADS * HEAD, D), (HEADS * HEAD) ** -0.5, 0.125, ((0, 8),)),
        "kv_cache": draw_kv_cache(jax.random.fold_in(seeds[8], 71), 0),
        "lengths": draw_lengths(jax.random.fold_in(seeds[8], 71), 0),
        "page_frame": draw_page_frame(jax.random.fold_in(seeds[8], 71), 0),
        "dest_frame": draw_dest_frame(jax.random.fold_in(seeds[8], 71), 0),
    }


LOW_SCORE = -1e30


def reference(tokens, w_query, w_keyval, w_out, kv_cache, lengths, page_frame, dest_frame):
    group_size = HEADS // KV_HEADS
    copy_step = COPIES // KV_HEADS
    score_scale = HEAD ** -0.5
    flat_rows = tokens.reshape(REQ * TOK, D)
    queries = jnp.dot(flat_rows, w_query, preferred_element_type=jnp.float32).astype(jnp.bfloat16).reshape(REQ, TOK, HEADS * HEAD)
    keyval = jnp.dot(flat_rows, w_keyval, preferred_element_type=jnp.float32).astype(jnp.bfloat16).reshape(REQ, TOK, KV_HEADS, 2 * HEAD)
    token_ids = jnp.arange(TOK, dtype=jnp.int32)
    slot_ids = jnp.arange(PAGES, dtype=jnp.int32)[:, None] * SLOTS + jnp.arange(SLOTS, dtype=jnp.int32)[None, :]
    causal = token_ids[:, None] >= token_ids[None, :]

    def one_request(inputs):
        request_queries, request_keyval, frames, length = inputs
        page_rows = kv_cache[frames][:, ::copy_step].astype(jnp.float32)
        query_heads = request_queries.reshape(TOK, KV_HEADS, group_size, HEAD).astype(jnp.float32)
        scores = jnp.einsum("tgqd,pgsd->tgqps", query_heads, page_rows[..., :HEAD]) * score_scale
        visible = (slot_ids[None] < length) & (slot_ids[None] >= length + token_ids[:, None, None] - WINDOW + 1)
        visible = visible[:, None, None]
        scores = jnp.where(visible, scores, LOW_SCORE)
        peak_vals = jnp.max(scores, axis=-1)
        weights = jnp.where(visible, jnp.exp(scores - peak_vals[..., None]), 0.0).astype(jnp.bfloat16).astype(jnp.float32)
        totals = jnp.sum(weights, axis=-1)
        partials = jnp.einsum("tgqps,pgsd->tgqpd", weights, page_rows[..., HEAD:])
        new_rows = request_keyval.astype(jnp.float32)
        new_scores = jnp.einsum("tgqd,ugd->tgqu", query_heads, new_rows[..., :HEAD]) * score_scale
        new_visible = causal[:, None, None, :]
        new_scores = jnp.where(new_visible, new_scores, LOW_SCORE)
        new_peak = jnp.max(new_scores, axis=-1)
        new_weights = jnp.where(new_visible, jnp.exp(new_scores - new_peak[..., None]), 0.0).astype(jnp.bfloat16).astype(jnp.float32)
        new_total = jnp.sum(new_weights, axis=-1)
        new_partial = jnp.einsum("tgqu,ugd->tgqd", new_weights, new_rows[..., HEAD:])
        top_peak = jnp.maximum(jnp.max(peak_vals, axis=-1), new_peak)
        old_scale = jnp.exp(peak_vals - top_peak[..., None])
        new_scale = jnp.exp(new_peak - top_peak)
        denominator = jnp.sum(old_scale * totals, axis=-1) + new_scale * new_total
        numerator = jnp.sum(old_scale[..., None] * partials, axis=-2) + new_scale[..., None] * new_partial
        return (numerator / denominator[..., None]).reshape(TOK, HEADS * HEAD).astype(jnp.bfloat16)

    attended = lax.map(one_request, (queries, keyval, page_frame, lengths))
    hidden = jnp.dot(attended.reshape(REQ * TOK, HEADS * HEAD), w_out, preferred_element_type=jnp.float32).astype(jnp.bfloat16).reshape(REQ, TOK, D)
    flat_old = page_frame.reshape(-1)
    flat_new = dest_frame.reshape(-1)
    moved_cache = kv_cache.at[flat_new].set(kv_cache[flat_old])
    slot_pos = (lengths[:, None] + token_ids[None, :]).astype(jnp.int32)
    frame_of = jnp.take_along_axis(dest_frame, (slot_pos // SLOTS).astype(jnp.int32), axis=1)
    copy_ids = jnp.arange(COPIES, dtype=jnp.int32)
    new_values = keyval[:, :, copy_ids // copy_step]
    new_cache = moved_cache.at[frame_of[:, :, None], copy_ids[None, None, :], (slot_pos % SLOTS)[:, :, None]].set(new_values)
    return hidden, new_cache
```

```python
import jax
import jax.numpy as jnp
from jax import lax
from jax.sharding import PartitionSpec as P

WINDOW = 2048
LOW_SCORE = -1e30
HIGH = lax.Precision.HIGHEST


def page_blocks(store, page_frame, lengths, queries, seq_index):
    frame_total, slot_count, row_width = store.shape
    head_dim = row_width // 2
    req_total, token_count, heads_here, _ = queries.shape
    page_count = page_frame.shape[1]
    flat = page_frame.reshape(-1)
    page_ids = jnp.arange(flat.shape[0], dtype=jnp.int32)
    here = seq_index * frame_total + jnp.arange(frame_total, dtype=jnp.int32)
    matches = flat[None, :] == here[:, None]
    owner = jnp.sum(jnp.where(matches, page_ids[None, :], 0), axis=1)
    occupied = jnp.any(matches, axis=1)
    request = owner // page_count
    page_no = owner % page_count
    length = lengths[request]
    frame_q = queries[request]
    scores = jnp.einsum(
        "fthd,fsd->fths", frame_q, store[..., :head_dim], preferred_element_type=jnp.float32
    ) * head_dim ** (-0.5)
    token_ids = jnp.arange(token_count, dtype=jnp.int32)
    slot_pos = page_no[:, None] * slot_count + jnp.arange(slot_count, dtype=jnp.int32)[None, :]
    visible = (
        occupied[:, None, None]
        & (slot_pos[:, None, :] < length[:, None, None])
        & (slot_pos[:, None, :] >= (length[:, None] + token_ids[None, :] - WINDOW + 1)[:, :, None])
    )[:, :, None, :]
    scores = jnp.where(visible, scores, LOW_SCORE)
    peak = jnp.max(scores, axis=-1)
    weights = jnp.where(visible, jnp.exp(scores - peak[..., None]), 0.0).astype(jnp.bfloat16)
    total = jnp.sum(weights.astype(jnp.float32), axis=-1)
    partial = jnp.einsum(
        "fths,fsd->fthd", weights, store[..., head_dim:], preferred_element_type=jnp.float32
    )
    onehot = request[None, :] == jnp.arange(req_total, dtype=jnp.int32)[:, None]
    local_peak = jnp.max(jnp.where(onehot[:, :, None, None], peak[None], LOW_SCORE), axis=1)
    scale = jnp.exp(peak - local_peak[request])
    onehot_f = onehot.astype(jnp.float32)
    local_total = jnp.einsum("rf,fth->rth", onehot_f, scale * total, precision=HIGH)
    local_partial = jnp.einsum("rf,fthd->rthd", onehot_f, scale[..., None] * partial, precision=HIGH)
    return jnp.concatenate(
        [local_peak[..., None], local_total[..., None], local_partial], axis=-1
    )


def migrate(frame_store, flat_old, flat_new, seq_index, seq_count):
    frame_total = frame_store.shape[0]
    old_device = flat_old // frame_total
    old_local = flat_old % frame_total
    new_device = flat_new // frame_total
    new_local = flat_new % frame_total
    moving = flat_old != flat_new
    peer_ids = jnp.arange(seq_count, dtype=jnp.int32)[:, None]
    leaving = (
        moving[None, :] & (old_device == seq_index)[None, :] & (new_device[None, :] == peer_ids)
    )
    send_local = jnp.sum(jnp.where(leaving, old_local[None, :], 0), axis=1)
    send_any = jnp.any(leaving, axis=1)
    outgoing = jnp.where(
        send_any[:, None, None], frame_store[send_local], jnp.zeros_like(frame_store[send_local])
    )
    incoming = lax.all_to_all(outgoing, "seq", split_axis=0, concat_axis=0, tiled=True)
    arriving = (
        moving[None, :] & (new_device == seq_index)[None, :] & (old_device[None, :] == peer_ids)
    )
    recv_local = jnp.sum(jnp.where(arriving, new_local[None, :], 0), axis=1)
    recv_any = jnp.any(arriving, axis=1)
    target = jnp.where(recv_any, recv_local, frame_total)
    return frame_store.at[target].set(incoming, mode="drop")


def local(tokens, w_query, w_keyval, w_out, kv_cache, lengths, page_frame, dest_frame):
    seq_index = lax.axis_index("seq")
    seq_count = lax.axis_size("seq")
    tp_index = lax.axis_index("tp")
    tp_count = lax.axis_size("tp")
    req_here, token_count, model_width = tokens.shape
    req_total = req_here * seq_count
    head_dim = kv_cache.shape[3] // 2
    kv_heads = w_keyval.shape[1] // (2 * head_dim)
    query_cols = w_query.shape[1]
    heads_here = query_cols // head_dim
    kv_group = tp_index // (tp_count // kv_heads)
    kv_columns = lax.dynamic_slice_in_dim(w_keyval, kv_group * 2 * head_dim, 2 * head_dim, 1)
    rows = tokens.reshape(-1, model_width)
    query_here = jnp.dot(rows, w_query, preferred_element_type=jnp.float32).astype(jnp.bfloat16)
    keyval_here = jnp.dot(rows, kv_columns, preferred_element_type=jnp.float32).astype(jnp.bfloat16)
    joined = jnp.concatenate([query_here, keyval_here], axis=1).reshape(
        req_here, token_count, query_cols + 2 * head_dim
    )
    joined_all = lax.all_gather(joined, "seq", axis=0, tiled=True)
    queries = joined_all[..., :query_cols].reshape(req_total, token_count, heads_here, head_dim)
    keyval = joined_all[..., query_cols:]
    frame_store = kv_cache[:, 0]

    blocks = page_blocks(frame_store, page_frame, lengths, queries, seq_index)
    arrived = lax.all_to_all(blocks, "seq", split_axis=0, concat_axis=0, tiled=True)
    arrived = arrived.reshape(seq_count, req_here, token_count, heads_here, head_dim + 2)
    src_peak = arrived[..., 0]
    src_total = arrived[..., 1]
    src_partial = arrived[..., 2:]

    own_q = query_here.reshape(req_here, token_count, heads_here, head_dim)
    own_kv = keyval_here.reshape(req_here, token_count, 2 * head_dim)
    token_ids = jnp.arange(token_count, dtype=jnp.int32)
    causal = (token_ids[:, None] >= token_ids[None, :])[None, :, None, :]
    new_scores = jnp.einsum(
        "rtqd,rud->rtqu", own_q, own_kv[..., :head_dim], preferred_element_type=jnp.float32
    ) * head_dim ** (-0.5)
    new_scores = jnp.where(causal, new_scores, LOW_SCORE)
    new_peak = jnp.max(new_scores, axis=-1)
    new_weights = jnp.where(causal, jnp.exp(new_scores - new_peak[..., None]), 0.0).astype(
        jnp.bfloat16
    )
    new_total = jnp.sum(new_weights.astype(jnp.float32), axis=-1)
    new_partial = jnp.einsum(
        "rtqu,rud->rtqd", new_weights, own_kv[..., head_dim:], preferred_element_type=jnp.float32
    )
    top = jnp.maximum(jnp.max(src_peak, axis=0), new_peak)
    src_scale = jnp.exp(src_peak - top[None])
    new_scale = jnp.exp(new_peak - top)
    denominator = jnp.sum(src_scale * src_total, axis=0) + new_scale * new_total
    numerator = jnp.sum(src_scale[..., None] * src_partial, axis=0) + new_scale[..., None] * new_partial
    attended = (numerator / denominator[..., None]).astype(jnp.bfloat16)
    out_term = jnp.dot(
        attended.reshape(req_here * token_count, query_cols),
        w_out,
        preferred_element_type=jnp.float32,
    ).reshape(req_here, token_count, -1)
    hidden = lax.psum_scatter(out_term, "tp", scatter_dimension=2, tiled=True).astype(jnp.bfloat16)

    flat_old = page_frame.reshape(-1)
    flat_new = dest_frame.reshape(-1)
    moved_store = migrate(frame_store, flat_old, flat_new, seq_index, seq_count)
    frame_total, slot_count = (frame_store.shape[0], frame_store.shape[1])
    slot_pos = lengths[:, None] + token_ids[None, :]
    frame_of = jnp.take_along_axis(dest_frame, slot_pos // slot_count, axis=1)
    target = jnp.where(frame_of // frame_total == seq_index, frame_of % frame_total, frame_total)
    new_store = moved_store.at[target, slot_pos % slot_count].set(keyval, mode="drop")
    return (hidden, new_store[:, None])


def solution(mesh):
    placed = (
        P("seq", None, None),
        P(None, "tp"),
        P(),
        P("tp", None),
        P("seq", "tp", None, None),
        P(),
        P(),
        P(),
    )
    return jax.shard_map(
        local,
        mesh=mesh,
        in_specs=placed,
        out_specs=(P("seq", None, "tp"), P("seq", "tp", None, None)),
        check_vma=False,
    )
```

```python
import jax
import jax.numpy as jnp
from jax import lax
from jax.sharding import PartitionSpec as P

WINDOW = 2048
LOW_SCORE = -1e30
HIGH = lax.Precision.HIGHEST


def page_blocks(store, page_frame, lengths, queries, seq_index):
    frame_total, slot_count, row_width = store.shape
    head_dim = row_width // 2
    req_total, token_count, heads_here, _ = queries.shape
    page_count = page_frame.shape[1]
    flat = page_frame.reshape(-1)
    page_ids = jnp.arange(flat.shape[0], dtype=jnp.int32)
    here = seq_index * frame_total + jnp.arange(frame_total, dtype=jnp.int32)
    matches = flat[None, :] == here[:, None]
    owner = jnp.sum(jnp.where(matches, page_ids[None, :], 0), axis=1)
    occupied = jnp.any(matches, axis=1)
    request = owner // page_count
    page_no = owner % page_count
    length = lengths[request]
    frame_q = queries[request]
    keys_t = jnp.swapaxes(store[..., :head_dim], 1, 2)
    scores = jnp.einsum(
        "fds,fthd->fsth", keys_t, frame_q, preferred_element_type=jnp.float32
    ) * head_dim ** (-0.5)
    token_ids = jnp.arange(token_count, dtype=jnp.int32)
    slot_pos = page_no[:, None] * slot_count + jnp.arange(slot_count, dtype=jnp.int32)[None, :]
    visible = (
        occupied[:, None, None]
        & (slot_pos[:, :, None] < length[:, None, None])
        & (slot_pos[:, :, None] >= (length[:, None] + token_ids[None, :] - WINDOW + 1)[:, None, :])
    )[..., None]
    scores = jnp.where(visible, scores, LOW_SCORE)
    peak = jnp.max(scores, axis=1)
    weights = jnp.where(visible, jnp.exp(scores - peak[:, None]), 0.0).astype(jnp.bfloat16)
    total = jnp.sum(weights.astype(jnp.float32), axis=1)
    partial = jnp.einsum(
        "fsth,fsd->fthd", weights, store[..., head_dim:], preferred_element_type=jnp.float32
    )
    onehot = request[None, :] == jnp.arange(req_total, dtype=jnp.int32)[:, None]
    local_peak = jnp.max(jnp.where(onehot[:, :, None, None], peak[None], LOW_SCORE), axis=1)
    scale = jnp.exp(peak - local_peak[request])
    onehot_f = onehot.astype(jnp.float32)
    local_total = jnp.einsum("rf,fth->rth", onehot_f, scale * total, precision=HIGH)
    local_partial = jnp.einsum("rf,fthd->rthd", onehot_f, scale[..., None] * partial, precision=HIGH)
    return jnp.concatenate(
        [local_peak[..., None], local_total[..., None], local_partial], axis=-1
    )


def rebuild(frame_store, flat_old, flat_new, lengths, keyval, seq_index, seq_count, token_count):
    frame_total, slot_count, _ = frame_store.shape
    page_count = flat_new.shape[0] // lengths.shape[0]
    old_device = flat_old // frame_total
    old_local = flat_old % frame_total
    new_device = flat_new // frame_total
    moving = flat_old != flat_new
    peer_ids = jnp.arange(seq_count, dtype=jnp.int32)[:, None]
    leaving = (
        moving[None, :] & (old_device == seq_index)[None, :] & (new_device[None, :] == peer_ids)
    )
    send_local = jnp.sum(jnp.where(leaving, old_local[None, :], 0), axis=1)
    send_any = jnp.any(leaving, axis=1)
    outgoing = jnp.where(
        send_any[:, None, None], frame_store[send_local], jnp.zeros_like(frame_store[send_local])
    )
    incoming = lax.all_to_all(outgoing, "seq", split_axis=0, concat_axis=0, tiled=True)
    page_ids = jnp.arange(flat_new.shape[0], dtype=jnp.int32)
    here = seq_index * frame_total + jnp.arange(frame_total, dtype=jnp.int32)
    matches = flat_new[None, :] == here[:, None]
    owner = jnp.sum(jnp.where(matches, page_ids[None, :], 0), axis=1)
    occupied = jnp.any(matches, axis=1)
    came_from = flat_old[owner]
    arrived = occupied & (came_from != here)
    source = came_from // frame_total
    request = owner // page_count
    page_no = owner % page_count
    token_at = (
        page_no[:, None] * slot_count
        + jnp.arange(slot_count, dtype=jnp.int32)[None, :]
        - lengths[request][:, None]
    )
    fresh = occupied[:, None] & (token_at >= 0) & (token_at < token_count)
    rows_new = keyval[request]
    value = jnp.broadcast_to(rows_new[:, 0][:, None, :], frame_store.shape)
    for t in range(1, token_count):
        value = jnp.where((token_at == t)[..., None], rows_new[:, t][:, None, :], value)
    moved = jnp.where(arrived[:, None, None], incoming[source], frame_store)
    return jnp.where(fresh[..., None], value, moved)


def local(tokens, w_query, w_keyval, w_out, kv_cache, lengths, page_frame, dest_frame):
    seq_index = lax.axis_index("seq")
    seq_count = lax.axis_size("seq")
    tp_index = lax.axis_index("tp")
    tp_count = lax.axis_size("tp")
    req_here, token_count, model_width = tokens.shape
    req_total = req_here * seq_count
    head_dim = kv_cache.shape[3] // 2
    kv_heads = w_keyval.shape[1] // (2 * head_dim)
    query_cols = w_query.shape[1]
    heads_here = query_cols // head_dim
    kv_group = tp_index // (tp_count // kv_heads)
    kv_columns = lax.dynamic_slice_in_dim(w_keyval, kv_group * 2 * head_dim, 2 * head_dim, 1)
    rows = tokens.reshape(-1, model_width)
    query_here = jnp.dot(rows, w_query, preferred_element_type=jnp.float32).astype(jnp.bfloat16)
    keyval_here = jnp.dot(rows, kv_columns, preferred_element_type=jnp.float32).astype(jnp.bfloat16)
    joined = jnp.concatenate([query_here, keyval_here], axis=1).reshape(
        req_here, token_count, query_cols + 2 * head_dim
    )
    joined_all = lax.all_gather(joined, "seq", axis=0, tiled=True)
    queries = joined_all[..., :query_cols].reshape(req_total, token_count, heads_here, head_dim)
    keyval = joined_all[..., query_cols:]
    frame_store = kv_cache[:, 0]

    blocks = page_blocks(frame_store, page_frame, lengths, queries, seq_index)
    arrived = lax.all_to_all(blocks, "seq", split_axis=0, concat_axis=0, tiled=True)
    arrived = arrived.reshape(seq_count, req_here, token_count, heads_here, head_dim + 2)
    src_peak = arrived[..., 0]
    src_total = arrived[..., 1]
    src_partial = arrived[..., 2:]

    own_q = query_here.reshape(req_here, token_count, heads_here, head_dim)
    own_kv = keyval_here.reshape(req_here, token_count, 2 * head_dim)
    token_ids = jnp.arange(token_count, dtype=jnp.int32)
    causal = (token_ids[:, None] >= token_ids[None, :])[None, :, None, :]
    new_scores = jnp.einsum(
        "rtqd,rud->rtqu", own_q, own_kv[..., :head_dim], preferred_element_type=jnp.float32
    ) * head_dim ** (-0.5)
    new_scores = jnp.where(causal, new_scores, LOW_SCORE)
    new_peak = jnp.max(new_scores, axis=-1)
    new_weights = jnp.where(causal, jnp.exp(new_scores - new_peak[..., None]), 0.0).astype(
        jnp.bfloat16
    )
    new_total = jnp.sum(new_weights.astype(jnp.float32), axis=-1)
    new_partial = jnp.einsum(
        "rtqu,rud->rtqd", new_weights, own_kv[..., head_dim:], preferred_element_type=jnp.float32
    )
    top = jnp.maximum(jnp.max(src_peak, axis=0), new_peak)
    src_scale = jnp.exp(src_peak - top[None])
    new_scale = jnp.exp(new_peak - top)
    denominator = jnp.sum(src_scale * src_total, axis=0) + new_scale * new_total
    numerator = jnp.sum(src_scale[..., None] * src_partial, axis=0) + new_scale[..., None] * new_partial
    attended = (numerator / denominator[..., None]).astype(jnp.bfloat16)
    out_term = jnp.dot(
        attended.reshape(req_here * token_count, query_cols),
        w_out,
        preferred_element_type=jnp.float32,
    ).reshape(req_here, token_count, -1)
    col_count = out_term.shape[2] // tp_count
    pieces = out_term.reshape(req_here * token_count, tp_count, col_count).transpose(1, 0, 2)
    gathered = lax.all_to_all(pieces, "tp", split_axis=0, concat_axis=0, tiled=True)
    hidden = jnp.sum(gathered, axis=0).astype(jnp.bfloat16).reshape(req_here, token_count, col_count)

    flat_old = page_frame.reshape(-1)
    flat_new = dest_frame.reshape(-1)
    new_store = rebuild(frame_store, flat_old, flat_new, lengths, keyval, seq_index, seq_count, token_count)
    return (hidden, new_store[:, None])


def solution(mesh):
    placed = (
        P("seq", None, None),
        P(None, "tp"),
        P(),
        P("tp", None),
        P("seq", "tp", None, None),
        P(),
        P(),
        P(),
    )
    return jax.shard_map(
        local,
        mesh=mesh,
        in_specs=placed,
        out_specs=(P("seq", None, "tp"), P("seq", "tp", None, None)),
        check_vma=False,
    )
```

```python
import jax
import jax.numpy as jnp
from jax import lax
from jax.sharding import PartitionSpec as P

WINDOW = 2048
LOW_SCORE = -1e30
HIGH = lax.Precision.HIGHEST


def page_blocks(store, page_frame, lengths, queries, seq_index):
    frame_total, slot_count, row_width = store.shape
    head_dim = row_width // 2
    req_total, token_count, heads_here, _ = queries.shape
    page_count = page_frame.shape[1]
    flat = page_frame.reshape(-1)
    page_ids = jnp.arange(flat.shape[0], dtype=jnp.int32)
    here = seq_index * frame_total + jnp.arange(frame_total, dtype=jnp.int32)
    matches = flat[None, :] == here[:, None]
    owner = jnp.sum(jnp.where(matches, page_ids[None, :], 0), axis=1)
    occupied = jnp.any(matches, axis=1)
    request = owner // page_count
    page_no = owner % page_count
    length = lengths[request]
    frame_q = queries[request]
    keys_t = jnp.swapaxes(store[..., :head_dim], 1, 2)
    scores = jnp.einsum(
        "fds,fthd->fsth", keys_t, frame_q, preferred_element_type=jnp.float32
    ) * head_dim ** (-0.5)
    token_ids = jnp.arange(token_count, dtype=jnp.int32)
    slot_pos = page_no[:, None] * slot_count + jnp.arange(slot_count, dtype=jnp.int32)[None, :]
    visible = (
        occupied[:, None, None]
        & (slot_pos[:, :, None] < length[:, None, None])
        & (slot_pos[:, :, None] >= (length[:, None] + token_ids[None, :] - WINDOW + 1)[:, None, :])
    )[..., None]
    scores = jnp.where(visible, scores, LOW_SCORE)
    peak = jnp.max(scores, axis=1)
    weights = jnp.where(visible, jnp.exp(scores - peak[:, None]), 0.0).astype(jnp.bfloat16)
    total = jnp.sum(weights.astype(jnp.float32), axis=1)
    partial = jnp.einsum(
        "fsth,fsd->fthd", weights, store[..., head_dim:], preferred_element_type=jnp.float32
    )
    onehot = request[None, :] == jnp.arange(req_total, dtype=jnp.int32)[:, None]
    local_peak = jnp.max(jnp.where(onehot[:, :, None, None], peak[None], LOW_SCORE), axis=1)
    scale = jnp.exp(peak - local_peak[request])
    onehot_f = onehot.astype(jnp.float32)
    local_total = jnp.einsum("rf,fth->rth", onehot_f, scale * total, precision=HIGH)
    local_partial = jnp.einsum("rf,fthd->rthd", onehot_f, scale[..., None] * partial, precision=HIGH)
    return jnp.concatenate(
        [local_peak[..., None], local_total[..., None], local_partial], axis=-1
    )


def outgoing_pages(frame_store, flat_old, flat_new, seq_index, seq_count):
    frame_total = frame_store.shape[0]
    old_device = flat_old // frame_total
    old_local = flat_old % frame_total
    new_device = flat_new // frame_total
    moving = flat_old != flat_new
    peer_ids = jnp.arange(seq_count, dtype=jnp.int32)[:, None]
    leaving = (
        moving[None, :] & (old_device == seq_index)[None, :] & (new_device[None, :] == peer_ids)
    )
    send_local = jnp.sum(jnp.where(leaving, old_local[None, :], 0), axis=1)
    send_any = jnp.any(leaving, axis=1)
    return jnp.where(
        send_any[:, None, None], frame_store[send_local], jnp.zeros_like(frame_store[send_local])
    )


def rebuild(frame_store, incoming, flat_old, flat_new, lengths, keyval, seq_index, token_count):
    frame_total, slot_count, _ = frame_store.shape
    page_count = flat_new.shape[0] // lengths.shape[0]
    page_ids = jnp.arange(flat_new.shape[0], dtype=jnp.int32)
    here = seq_index * frame_total + jnp.arange(frame_total, dtype=jnp.int32)
    matches = flat_new[None, :] == here[:, None]
    owner = jnp.sum(jnp.where(matches, page_ids[None, :], 0), axis=1)
    occupied = jnp.any(matches, axis=1)
    came_from = flat_old[owner]
    arrived = occupied & (came_from != here)
    source = came_from // frame_total
    request = owner // page_count
    page_no = owner % page_count
    token_at = (
        page_no[:, None] * slot_count
        + jnp.arange(slot_count, dtype=jnp.int32)[None, :]
        - lengths[request][:, None]
    )
    fresh = occupied[:, None] & (token_at >= 0) & (token_at < token_count)
    rows_new = keyval[request]
    value = jnp.broadcast_to(rows_new[:, 0][:, None, :], frame_store.shape)
    for t in range(1, token_count):
        value = jnp.where((token_at == t)[..., None], rows_new[:, t][:, None, :], value)
    moved = jnp.where(arrived[:, None, None], incoming[source], frame_store)
    return jnp.where(fresh[..., None], value, moved)


def local(tokens, w_query, w_keyval, w_out, kv_cache, lengths, page_frame, dest_frame):
    seq_index = lax.axis_index("seq")
    seq_count = lax.axis_size("seq")
    tp_index = lax.axis_index("tp")
    tp_count = lax.axis_size("tp")
    req_here, token_count, model_width = tokens.shape
    req_total = req_here * seq_count
    head_dim = kv_cache.shape[3] // 2
    kv_heads = w_keyval.shape[1] // (2 * head_dim)
    query_cols = w_query.shape[1]
    heads_here = query_cols // head_dim
    kv_group = tp_index // (tp_count // kv_heads)
    kv_columns = lax.dynamic_slice_in_dim(w_keyval, kv_group * 2 * head_dim, 2 * head_dim, 1)
    rows = tokens.reshape(-1, model_width)
    query_here = jnp.dot(rows, w_query, preferred_element_type=jnp.float32).astype(jnp.bfloat16)
    keyval_here = jnp.dot(rows, kv_columns, preferred_element_type=jnp.float32).astype(jnp.bfloat16)
    joined = jnp.concatenate([query_here, keyval_here], axis=1).reshape(
        req_here, token_count, query_cols + 2 * head_dim
    )
    frame_store = kv_cache[:, 0]
    frame_total, slot_count, row_width = frame_store.shape
    flat_old = page_frame.reshape(-1)
    flat_new = dest_frame.reshape(-1)
    outgoing = outgoing_pages(frame_store, flat_old, flat_new, seq_index, seq_count)
    page_size = slot_count * row_width
    own_size = req_here * token_count * (query_cols + 2 * head_dim)
    send = jnp.concatenate(
        [
            outgoing.reshape(seq_count, page_size),
            jnp.broadcast_to(joined.reshape(1, own_size), (seq_count, own_size)),
        ],
        axis=1,
    )
    received = lax.all_to_all(send, "seq", split_axis=0, concat_axis=0, tiled=True)
    incoming = received[:, :page_size].reshape(seq_count, slot_count, row_width)
    joined_all = received[:, page_size:].reshape(req_total, token_count, query_cols + 2 * head_dim)
    queries = joined_all[..., :query_cols].reshape(req_total, token_count, heads_here, head_dim)
    keyval = joined_all[..., query_cols:]

    blocks = page_blocks(frame_store, page_frame, lengths, queries, seq_index)
    arrived = lax.all_to_all(blocks, "seq", split_axis=0, concat_axis=0, tiled=True)
    arrived = arrived.reshape(seq_count, req_here, token_count, heads_here, head_dim + 2)
    src_peak = arrived[..., 0]
    src_total = arrived[..., 1]
    src_partial = arrived[..., 2:]

    own_q = query_here.reshape(req_here, token_count, heads_here, head_dim)
    own_kv = keyval_here.reshape(req_here, token_count, 2 * head_dim)
    token_ids = jnp.arange(token_count, dtype=jnp.int32)
    causal = (token_ids[:, None] >= token_ids[None, :])[None, :, None, :]
    new_scores = jnp.einsum(
        "rtqd,rud->rtqu", own_q, own_kv[..., :head_dim], preferred_element_type=jnp.float32
    ) * head_dim ** (-0.5)
    new_scores = jnp.where(causal, new_scores, LOW_SCORE)
    new_peak = jnp.max(new_scores, axis=-1)
    new_weights = jnp.where(causal, jnp.exp(new_scores - new_peak[..., None]), 0.0).astype(
        jnp.bfloat16
    )
    new_total = jnp.sum(new_weights.astype(jnp.float32), axis=-1)
    new_partial = jnp.einsum(
        "rtqu,rud->rtqd", new_weights, own_kv[..., head_dim:], preferred_element_type=jnp.float32
    )
    top = jnp.maximum(jnp.max(src_peak, axis=0), new_peak)
    src_scale = jnp.exp(src_peak - top[None])
    new_scale = jnp.exp(new_peak - top)
    denominator = jnp.sum(src_scale * src_total, axis=0) + new_scale * new_total
    numerator = jnp.sum(src_scale[..., None] * src_partial, axis=0) + new_scale[..., None] * new_partial
    attended = (numerator / denominator[..., None]).astype(jnp.bfloat16)
    out_term = jnp.dot(
        attended.reshape(req_here * token_count, query_cols),
        w_out,
        preferred_element_type=jnp.float32,
    ).reshape(req_here, token_count, -1)
    col_count = out_term.shape[2] // tp_count
    pieces = out_term.reshape(req_here * token_count, tp_count, col_count).transpose(1, 0, 2)
    gathered = lax.all_to_all(pieces, "tp", split_axis=0, concat_axis=0, tiled=True)
    hidden = jnp.sum(gathered, axis=0).astype(jnp.bfloat16).reshape(req_here, token_count, col_count)

    new_store = rebuild(
        lax.optimization_barrier(frame_store), incoming, flat_old, flat_new, lengths, keyval, seq_index, token_count
    )
    return (hidden, new_store[:, None])


def solution(mesh):
    placed = (
        P("seq", None, None),
        P(None, "tp"),
        P(),
        P("tp", None),
        P("seq", "tp", None, None),
        P(),
        P(),
        P(),
    )
    return jax.shard_map(
        local,
        mesh=mesh,
        in_specs=placed,
        out_specs=(P("seq", None, "tp"), P("seq", "tp", None, None)),
        check_vma=False,
    )
```

```python
import jax
import jax.numpy as jnp
from jax import lax
from jax.sharding import PartitionSpec as P

WINDOW = 2048
LOW_SCORE = -1e30
HIGH = lax.Precision.HIGHEST


def page_blocks(store, page_frame, lengths, queries, seq_index):
    frame_total, slot_count, row_width = store.shape
    head_dim = row_width // 2
    req_total, token_count, heads_here, _ = queries.shape
    page_count = page_frame.shape[1]
    flat = page_frame.reshape(-1)
    page_ids = jnp.arange(flat.shape[0], dtype=jnp.int32)
    here = seq_index * frame_total + jnp.arange(frame_total, dtype=jnp.int32)
    matches = flat[None, :] == here[:, None]
    owner = jnp.sum(jnp.where(matches, page_ids[None, :], 0), axis=1)
    occupied = jnp.any(matches, axis=1)
    request = owner // page_count
    page_no = owner % page_count
    length = lengths[request]
    frame_q = queries[request]
    keys_t = jnp.swapaxes(store[..., :head_dim], 1, 2)
    scores = jnp.einsum(
        "fds,fthd->fsth", keys_t, frame_q, preferred_element_type=jnp.float32
    ) * head_dim ** (-0.5)
    token_ids = jnp.arange(token_count, dtype=jnp.int32)
    slot_pos = page_no[:, None] * slot_count + jnp.arange(slot_count, dtype=jnp.int32)[None, :]
    visible = (
        occupied[:, None, None]
        & (slot_pos[:, :, None] < length[:, None, None])
        & (slot_pos[:, :, None] >= (length[:, None] + token_ids[None, :] - WINDOW + 1)[:, None, :])
    )[..., None]
    scores = jnp.where(visible, scores, LOW_SCORE)
    peak = jnp.max(scores, axis=1)
    weights = jnp.where(visible, jnp.exp(scores - peak[:, None]), 0.0).astype(jnp.bfloat16)
    total = jnp.sum(weights.astype(jnp.float32), axis=1)
    partial = jnp.einsum(
        "fsth,fsd->fthd", weights, store[..., head_dim:], preferred_element_type=jnp.float32
    )
    onehot = request[None, :] == jnp.arange(req_total, dtype=jnp.int32)[:, None]
    local_peak = jnp.max(jnp.where(onehot[:, :, None, None], peak[None], LOW_SCORE), axis=1)
    scale = jnp.exp(peak - local_peak[request])
    onehot_f = onehot.astype(jnp.float32)
    local_total = jnp.einsum("rf,fth->rth", onehot_f, scale * total, precision=HIGH)
    local_partial = jnp.einsum("rf,fthd->rthd", onehot_f, scale[..., None] * partial, precision=HIGH)
    return jnp.concatenate(
        [local_peak[..., None], local_total[..., None], local_partial], axis=-1
    )


def outgoing_pages(frame_store, flat_old, flat_new, seq_index, seq_count):
    frame_total = frame_store.shape[0]
    old_device = flat_old // frame_total
    old_local = flat_old % frame_total
    new_device = flat_new // frame_total
    moving = flat_old != flat_new
    peer_ids = jnp.arange(seq_count, dtype=jnp.int32)[:, None]
    leaving = (
        moving[None, :] & (old_device == seq_index)[None, :] & (new_device[None, :] == peer_ids)
    )
    send_local = jnp.sum(jnp.where(leaving, old_local[None, :], 0), axis=1)
    send_any = jnp.any(leaving, axis=1)
    return jnp.where(
        send_any[:, None, None], frame_store[send_local], jnp.zeros_like(frame_store[send_local])
    )


def rebuild(kv_cache, frame_store, incoming, flat_old, flat_new, lengths, keyval, seq_index, token_count):
    frame_total, slot_count, _ = frame_store.shape
    page_count = flat_new.shape[0] // lengths.shape[0]
    page_ids = jnp.arange(flat_new.shape[0], dtype=jnp.int32)
    here = seq_index * frame_total + jnp.arange(frame_total, dtype=jnp.int32)
    matches = flat_new[None, :] == here[:, None]
    owner = jnp.sum(jnp.where(matches, page_ids[None, :], 0), axis=1)
    occupied = jnp.any(matches, axis=1)
    request = owner // page_count
    page_no = owner % page_count
    token_at = (
        page_no[:, None] * slot_count
        + jnp.arange(slot_count, dtype=jnp.int32)[None, :]
        - lengths[request][:, None]
    )
    fresh = occupied[:, None] & (token_at >= 0) & (token_at < token_count)
    rows_new = keyval[request]
    value = jnp.broadcast_to(rows_new[:, 0][:, None, :], frame_store.shape)
    for t in range(1, token_count):
        value = jnp.where((token_at == t)[..., None], rows_new[:, t][:, None, :], value)
    old_device = flat_old // frame_total
    new_device = flat_new // frame_total
    seq_count = incoming.shape[0]
    peer_ids = jnp.arange(seq_count, dtype=jnp.int32)[:, None]
    arriving = (
        (flat_old != flat_new)[None, :]
        & (new_device == seq_index)[None, :]
        & (old_device[None, :] == peer_ids)
    )
    recv_local = jnp.sum(jnp.where(arriving, (flat_new % frame_total)[None, :], 0), axis=1)
    recv_any = jnp.any(arriving, axis=1)
    target = jnp.where(recv_any, recv_local, frame_total)
    moved = kv_cache.at[target].set(incoming[:, None], mode="drop")
    return jnp.where(fresh[:, None, :, None], value[:, None], moved)


def local(tokens, w_query, w_keyval, w_out, kv_cache, lengths, page_frame, dest_frame):
    seq_index = lax.axis_index("seq")
    seq_count = lax.axis_size("seq")
    tp_index = lax.axis_index("tp")
    tp_count = lax.axis_size("tp")
    req_here, token_count, model_width = tokens.shape
    req_total = req_here * seq_count
    head_dim = kv_cache.shape[3] // 2
    kv_heads = w_keyval.shape[1] // (2 * head_dim)
    query_cols = w_query.shape[1]
    heads_here = query_cols // head_dim
    kv_group = tp_index // (tp_count // kv_heads)
    kv_columns = lax.dynamic_slice_in_dim(w_keyval, kv_group * 2 * head_dim, 2 * head_dim, 1)
    rows = tokens.reshape(-1, model_width)
    query_here = jnp.dot(rows, w_query, preferred_element_type=jnp.float32).astype(jnp.bfloat16)
    keyval_here = jnp.dot(rows, kv_columns, preferred_element_type=jnp.float32).astype(jnp.bfloat16)
    joined = jnp.concatenate([query_here, keyval_here], axis=1).reshape(
        req_here, token_count, query_cols + 2 * head_dim
    )
    frame_store = kv_cache[:, 0]
    frame_total, slot_count, row_width = frame_store.shape
    flat_old = page_frame.reshape(-1)
    flat_new = dest_frame.reshape(-1)
    outgoing = outgoing_pages(frame_store, flat_old, flat_new, seq_index, seq_count)
    page_size = slot_count * row_width
    own_size = req_here * token_count * (query_cols + 2 * head_dim)
    send = jnp.concatenate(
        [
            outgoing.reshape(seq_count, page_size),
            jnp.broadcast_to(joined.reshape(1, own_size), (seq_count, own_size)),
        ],
        axis=1,
    )
    received = lax.all_to_all(send, "seq", split_axis=0, concat_axis=0, tiled=True)
    incoming = received[:, :page_size].reshape(seq_count, slot_count, row_width)
    joined_all = received[:, page_size:].reshape(req_total, token_count, query_cols + 2 * head_dim)
    queries = joined_all[..., :query_cols].reshape(req_total, token_count, heads_here, head_dim)
    keyval = joined_all[..., query_cols:]

    blocks = page_blocks(frame_store, page_frame, lengths, queries, seq_index)
    arrived = lax.all_to_all(blocks, "seq", split_axis=0, concat_axis=0, tiled=True)
    arrived = arrived.reshape(seq_count, req_here, token_count, heads_here, head_dim + 2)
    src_peak = arrived[..., 0]
    src_total = arrived[..., 1]
    src_partial = arrived[..., 2:]

    own_q = query_here.reshape(req_here, token_count, heads_here, head_dim)
    own_kv = keyval_here.reshape(req_here, token_count, 2 * head_dim)
    token_ids = jnp.arange(token_count, dtype=jnp.int32)
    causal = (token_ids[:, None] >= token_ids[None, :])[None, :, None, :]
    new_scores = jnp.einsum(
        "rtqd,rud->rtqu", own_q, own_kv[..., :head_dim], preferred_element_type=jnp.float32
    ) * head_dim ** (-0.5)
    new_scores = jnp.where(causal, new_scores, LOW_SCORE)
    new_peak = jnp.max(new_scores, axis=-1)
    new_weights = jnp.where(causal, jnp.exp(new_scores - new_peak[..., None]), 0.0).astype(
        jnp.bfloat16
    )
    new_total = jnp.sum(new_weights.astype(jnp.float32), axis=-1)
    new_partial = jnp.einsum(
        "rtqu,rud->rtqd", new_weights, own_kv[..., head_dim:], preferred_element_type=jnp.float32
    )
    top = jnp.maximum(jnp.max(src_peak, axis=0), new_peak)
    src_scale = jnp.exp(src_peak - top[None])
    new_scale = jnp.exp(new_peak - top)
    denominator = jnp.sum(src_scale * src_total, axis=0) + new_scale * new_total
    numerator = jnp.sum(src_scale[..., None] * src_partial, axis=0) + new_scale[..., None] * new_partial
    attended = (numerator / denominator[..., None]).astype(jnp.bfloat16)
    out_term = jnp.dot(
        attended.reshape(req_here * token_count, query_cols),
        w_out,
        preferred_element_type=jnp.float32,
    ).reshape(req_here, token_count, -1)
    col_count = out_term.shape[2] // tp_count
    pieces = out_term.reshape(req_here * token_count, tp_count, col_count).transpose(1, 0, 2)
    gathered = lax.all_to_all(pieces, "tp", split_axis=0, concat_axis=0, tiled=True)
    hidden = jnp.sum(gathered, axis=0).astype(jnp.bfloat16).reshape(req_here, token_count, col_count)

    new_cache = rebuild(
        kv_cache, frame_store, incoming, flat_old, flat_new, lengths, keyval, seq_index, token_count
    )
    return (hidden, new_cache)


def solution(mesh):
    placed = (
        P("seq", None, None),
        P(None, "tp"),
        P(),
        P("tp", None),
        P("seq", "tp", None, None),
        P(),
        P(),
        P(),
    )
    return jax.shard_map(
        local,
        mesh=mesh,
        in_specs=placed,
        out_specs=(P("seq", None, "tp"), P("seq", "tp", None, None)),
        check_vma=False,
    )
```

```python
import jax
import jax.numpy as jnp
from jax import lax
from jax.sharding import PartitionSpec as P

WINDOW = 2048
LOW_SCORE = -1e30
HIGH = lax.Precision.HIGHEST


def page_blocks(store, page_frame, lengths, queries, seq_index):
    frame_total, slot_count, row_width = store.shape
    head_dim = row_width // 2
    req_total, token_count, heads_here, _ = queries.shape
    page_count = page_frame.shape[1]
    flat = page_frame.reshape(-1)
    page_ids = jnp.arange(flat.shape[0], dtype=jnp.int32)
    here = seq_index * frame_total + jnp.arange(frame_total, dtype=jnp.int32)
    matches = flat[None, :] == here[:, None]
    owner = jnp.sum(jnp.where(matches, page_ids[None, :], 0), axis=1)
    occupied = jnp.any(matches, axis=1)
    request = owner // page_count
    page_no = owner % page_count
    length = lengths[request]
    frame_q = queries[request]
    keys_t = jnp.swapaxes(store[..., :head_dim], 1, 2)
    scores = jnp.einsum(
        "fds,fthd->fsth", keys_t, frame_q, preferred_element_type=jnp.float32
    ) * head_dim ** (-0.5)
    token_ids = jnp.arange(token_count, dtype=jnp.int32)
    slot_pos = page_no[:, None] * slot_count + jnp.arange(slot_count, dtype=jnp.int32)[None, :]
    visible = (
        occupied[:, None, None]
        & (slot_pos[:, :, None] < length[:, None, None])
        & (slot_pos[:, :, None] >= (length[:, None] + token_ids[None, :] - WINDOW + 1)[:, None, :])
    )[..., None]
    scores = jnp.where(visible, scores, LOW_SCORE)
    peak = jnp.max(scores, axis=1)
    weights = jnp.where(visible, jnp.exp(scores - peak[:, None]), 0.0).astype(jnp.bfloat16)
    total = jnp.sum(weights.astype(jnp.float32), axis=1)
    partial = jnp.einsum(
        "fsth,fsd->fthd", weights, store[..., head_dim:], preferred_element_type=jnp.float32
    )
    onehot = request[None, :] == jnp.arange(req_total, dtype=jnp.int32)[:, None]
    local_peak = jnp.max(jnp.where(onehot[:, :, None, None], peak[None], LOW_SCORE), axis=1)
    scale = jnp.exp(peak - local_peak[request])
    onehot_f = onehot.astype(jnp.float32)
    local_total = jnp.einsum("rf,fth->rth", onehot_f, scale * total, precision=HIGH)
    local_partial = jnp.einsum("rf,fthd->rthd", onehot_f, scale[..., None] * partial, precision=HIGH)
    return jnp.concatenate(
        [local_peak[..., None], local_total[..., None], local_partial], axis=-1
    )


def outgoing_pages(frame_store, flat_old, flat_new, seq_index, seq_count):
    frame_total = frame_store.shape[0]
    old_device = flat_old // frame_total
    old_local = flat_old % frame_total
    new_device = flat_new // frame_total
    moving = flat_old != flat_new
    peer_ids = jnp.arange(seq_count, dtype=jnp.int32)[:, None]
    leaving = (
        moving[None, :] & (old_device == seq_index)[None, :] & (new_device[None, :] == peer_ids)
    )
    send_local = jnp.sum(jnp.where(leaving, old_local[None, :], 0), axis=1)
    send_any = jnp.any(leaving, axis=1)
    return jnp.where(
        send_any[:, None, None], frame_store[send_local], jnp.zeros_like(frame_store[send_local])
    )


def rebuild(kv_cache, frame_store, incoming, flat_old, flat_new, lengths, keyval, seq_index, token_count):
    frame_total, slot_count, _ = frame_store.shape
    page_count = flat_new.shape[0] // lengths.shape[0]
    page_ids = jnp.arange(flat_new.shape[0], dtype=jnp.int32)
    here = seq_index * frame_total + jnp.arange(frame_total, dtype=jnp.int32)
    matches = flat_new[None, :] == here[:, None]
    owner = jnp.sum(jnp.where(matches, page_ids[None, :], 0), axis=1)
    occupied = jnp.any(matches, axis=1)
    request = owner // page_count
    page_no = owner % page_count
    token_at = (
        page_no[:, None] * slot_count
        + jnp.arange(slot_count, dtype=jnp.int32)[None, :]
        - lengths[request][:, None]
    )
    fresh = occupied[:, None] & (token_at >= 0) & (token_at < token_count)
    rows_new = keyval[request]
    pick = (token_at[..., None] == jnp.arange(token_count, dtype=jnp.int32)).astype(jnp.bfloat16)
    value = jnp.einsum(
        "fjt,ftc->fjc", pick, rows_new, preferred_element_type=jnp.float32
    ).astype(jnp.bfloat16)
    old_device = flat_old // frame_total
    new_device = flat_new // frame_total
    seq_count = incoming.shape[0]
    peer_ids = jnp.arange(seq_count, dtype=jnp.int32)[:, None]
    arriving = (
        (flat_old != flat_new)[None, :]
        & (new_device == seq_index)[None, :]
        & (old_device[None, :] == peer_ids)
    )
    recv_local = jnp.sum(jnp.where(arriving, (flat_new % frame_total)[None, :], 0), axis=1)
    recv_any = jnp.any(arriving, axis=1)
    target = jnp.where(recv_any, recv_local, frame_total)
    moved = kv_cache.at[target].set(incoming[:, None], mode="drop")
    return jnp.where(fresh[:, None, :, None], value[:, None], moved)


def local(tokens, w_query, w_keyval, w_out, kv_cache, lengths, page_frame, dest_frame):
    seq_index = lax.axis_index("seq")
    seq_count = lax.axis_size("seq")
    tp_index = lax.axis_index("tp")
    tp_count = lax.axis_size("tp")
    req_here, token_count, model_width = tokens.shape
    req_total = req_here * seq_count
    head_dim = kv_cache.shape[3] // 2
    kv_heads = w_keyval.shape[1] // (2 * head_dim)
    query_cols = w_query.shape[1]
    heads_here = query_cols // head_dim
    kv_group = tp_index // (tp_count // kv_heads)
    kv_columns = lax.dynamic_slice_in_dim(w_keyval, kv_group * 2 * head_dim, 2 * head_dim, 1)
    rows = tokens.reshape(-1, model_width)
    query_here = jnp.dot(rows, w_query, preferred_element_type=jnp.float32).astype(jnp.bfloat16)
    keyval_here = jnp.dot(rows, kv_columns, preferred_element_type=jnp.float32).astype(jnp.bfloat16)
    joined = jnp.concatenate([query_here, keyval_here], axis=1).reshape(
        req_here, token_count, query_cols + 2 * head_dim
    )
    frame_store = kv_cache[:, 0]
    frame_total, slot_count, row_width = frame_store.shape
    flat_old = page_frame.reshape(-1)
    flat_new = dest_frame.reshape(-1)
    outgoing = outgoing_pages(frame_store, flat_old, flat_new, seq_index, seq_count)
    page_size = slot_count * row_width
    own_size = req_here * token_count * (query_cols + 2 * head_dim)
    send = jnp.concatenate(
        [
            outgoing.reshape(seq_count, page_size),
            jnp.broadcast_to(joined.reshape(1, own_size), (seq_count, own_size)),
        ],
        axis=1,
    )
    received = lax.all_to_all(send, "seq", split_axis=0, concat_axis=0, tiled=True)
    incoming = received[:, :page_size].reshape(seq_count, slot_count, row_width)
    joined_all = received[:, page_size:].reshape(req_total, token_count, query_cols + 2 * head_dim)
    queries = joined_all[..., :query_cols].reshape(req_total, token_count, heads_here, head_dim)
    keyval = joined_all[..., query_cols:]

    blocks = page_blocks(frame_store, page_frame, lengths, queries, seq_index)
    arrived = lax.all_to_all(blocks, "seq", split_axis=0, concat_axis=0, tiled=True)
    arrived = arrived.reshape(seq_count, req_here, token_count, heads_here, head_dim + 2)
    src_peak = arrived[..., 0]
    src_total = arrived[..., 1]
    src_partial = arrived[..., 2:]

    own_q = query_here.reshape(req_here, token_count, heads_here, head_dim)
    own_kv = keyval_here.reshape(req_here, token_count, 2 * head_dim)
    token_ids = jnp.arange(token_count, dtype=jnp.int32)
    causal = (token_ids[:, None] >= token_ids[None, :])[None, :, None, :]
    new_scores = jnp.einsum(
        "rtqd,rud->rtqu", own_q, own_kv[..., :head_dim], preferred_element_type=jnp.float32
    ) * head_dim ** (-0.5)
    new_scores = jnp.where(causal, new_scores, LOW_SCORE)
    new_peak = jnp.max(new_scores, axis=-1)
    new_weights = jnp.where(causal, jnp.exp(new_scores - new_peak[..., None]), 0.0).astype(
        jnp.bfloat16
    )
    new_total = jnp.sum(new_weights.astype(jnp.float32), axis=-1)
    new_partial = jnp.einsum(
        "rtqu,rud->rtqd", new_weights, own_kv[..., head_dim:], preferred_element_type=jnp.float32
    )
    top = jnp.maximum(jnp.max(src_peak, axis=0), new_peak)
    src_scale = jnp.exp(src_peak - top[None])
    new_scale = jnp.exp(new_peak - top)
    denominator = jnp.sum(src_scale * src_total, axis=0) + new_scale * new_total
    numerator = jnp.sum(src_scale[..., None] * src_partial, axis=0) + new_scale[..., None] * new_partial
    attended = (numerator / denominator[..., None]).astype(jnp.bfloat16)
    out_term = jnp.dot(
        attended.reshape(req_here * token_count, query_cols),
        w_out,
        preferred_element_type=jnp.float32,
    ).reshape(req_here, token_count, -1)
    col_count = out_term.shape[2] // tp_count
    pieces = out_term.reshape(req_here * token_count, tp_count, col_count).transpose(1, 0, 2)
    gathered = lax.all_to_all(pieces, "tp", split_axis=0, concat_axis=0, tiled=True)
    hidden = jnp.sum(gathered, axis=0).astype(jnp.bfloat16).reshape(req_here, token_count, col_count)

    new_cache = rebuild(
        kv_cache, frame_store, incoming, flat_old, flat_new, lengths, keyval, seq_index, token_count
    )
    return (hidden, new_cache)


def solution(mesh):
    placed = (
        P("seq", None, None),
        P(None, "tp"),
        P(),
        P("tp", None),
        P("seq", "tp", None, None),
        P(),
        P(),
        P(),
    )
    return jax.shard_map(
        local,
        mesh=mesh,
        in_specs=placed,
        out_specs=(P("seq", None, "tp"), P("seq", "tp", None, None)),
        check_vma=False,
    )
```

```python
import jax
import jax.numpy as jnp
from jax import lax
from jax.sharding import PartitionSpec as P

WINDOW = 2048
LOW_SCORE = -1e30
HIGH = lax.Precision.HIGHEST


def page_blocks(store, page_frame, lengths, queries, seq_index):
    frame_total, slot_count, row_width = store.shape
    head_dim = row_width // 2
    req_total, token_count, heads_here, _ = queries.shape
    page_count = page_frame.shape[1]
    flat = page_frame.reshape(-1)
    page_ids = jnp.arange(flat.shape[0], dtype=jnp.int32)
    here = seq_index * frame_total + jnp.arange(frame_total, dtype=jnp.int32)
    matches = flat[None, :] == here[:, None]
    owner = jnp.sum(jnp.where(matches, page_ids[None, :], 0), axis=1)
    occupied = jnp.any(matches, axis=1)
    request = owner // page_count
    page_no = owner % page_count
    length = lengths[request]
    frame_q = queries[request]
    keys_t = jnp.swapaxes(store[..., :head_dim], 1, 2)
    scores = jnp.einsum(
        "fds,fthd->fsth", keys_t, frame_q, preferred_element_type=jnp.float32
    ) * head_dim ** (-0.5)
    token_ids = jnp.arange(token_count, dtype=jnp.int32)
    slot_pos = page_no[:, None] * slot_count + jnp.arange(slot_count, dtype=jnp.int32)[None, :]
    visible = (
        occupied[:, None, None]
        & (slot_pos[:, :, None] < length[:, None, None])
        & (slot_pos[:, :, None] >= (length[:, None] + token_ids[None, :] - WINDOW + 1)[:, None, :])
    )[..., None]
    scores = jnp.where(visible, scores, LOW_SCORE)
    peak = jnp.max(scores, axis=1)
    weights = jnp.where(visible, jnp.exp(scores - peak[:, None]), 0.0).astype(jnp.bfloat16)
    total = jnp.sum(weights.astype(jnp.float32), axis=1)
    partial = jnp.einsum(
        "fsth,fsd->fthd", weights, store[..., head_dim:], preferred_element_type=jnp.float32
    )
    onehot = request[None, :] == jnp.arange(req_total, dtype=jnp.int32)[:, None]
    local_peak = jnp.max(jnp.where(onehot[:, :, None, None], peak[None], LOW_SCORE), axis=1)
    scale = jnp.exp(peak - local_peak[request])
    onehot_f = onehot.astype(jnp.float32)
    local_total = jnp.einsum("rf,fth->rth", onehot_f, scale * total, precision=HIGH)
    local_partial = jnp.einsum("rf,fthd->rthd", onehot_f, scale[..., None] * partial, precision=HIGH)
    return jnp.concatenate(
        [local_peak[..., None], local_total[..., None], local_partial], axis=-1
    )


def outgoing_pages(frame_store, flat_old, flat_new, seq_index, seq_count):
    frame_total = frame_store.shape[0]
    old_device = flat_old // frame_total
    old_local = flat_old % frame_total
    new_device = flat_new // frame_total
    moving = flat_old != flat_new
    peer_ids = jnp.arange(seq_count, dtype=jnp.int32)[:, None]
    leaving = (
        moving[None, :] & (old_device == seq_index)[None, :] & (new_device[None, :] == peer_ids)
    )
    send_local = jnp.sum(jnp.where(leaving, old_local[None, :], 0), axis=1)
    send_any = jnp.any(leaving, axis=1)
    return jnp.where(
        send_any[:, None, None], frame_store[send_local], jnp.zeros_like(frame_store[send_local])
    )


def rebuild(kv_cache, frame_store, incoming, flat_old, flat_new, lengths, keyval, seq_index, token_count):
    frame_total, slot_count, _ = frame_store.shape
    page_count = flat_new.shape[0] // lengths.shape[0]
    page_ids = jnp.arange(flat_new.shape[0], dtype=jnp.int32)
    here = seq_index * frame_total + jnp.arange(frame_total, dtype=jnp.int32)
    matches = flat_new[None, :] == here[:, None]
    owner = jnp.sum(jnp.where(matches, page_ids[None, :], 0), axis=1)
    occupied = jnp.any(matches, axis=1)
    request = owner // page_count
    page_no = owner % page_count
    token_at = (
        page_no[:, None] * slot_count
        + jnp.arange(slot_count, dtype=jnp.int32)[None, :]
        - lengths[request][:, None]
    )
    fresh = occupied[:, None] & (token_at >= 0) & (token_at < token_count)
    rows_new = keyval[request]
    pick = (token_at[..., None] == jnp.arange(token_count, dtype=jnp.int32)).astype(jnp.bfloat16)
    value = jnp.einsum(
        "fjt,ftc->fjc", pick, rows_new, preferred_element_type=jnp.float32
    ).astype(jnp.bfloat16)
    old_device = flat_old // frame_total
    new_device = flat_new // frame_total
    seq_count = incoming.shape[0]
    peer_ids = jnp.arange(seq_count, dtype=jnp.int32)[:, None]
    arriving = (
        (flat_old != flat_new)[None, :]
        & (new_device == seq_index)[None, :]
        & (old_device[None, :] == peer_ids)
    )
    recv_local = jnp.sum(jnp.where(arriving, (flat_new % frame_total)[None, :], 0), axis=1)
    recv_any = jnp.any(arriving, axis=1)
    target = jnp.where(recv_any, recv_local, frame_total)
    moved = kv_cache.at[target].set(incoming[:, None], mode="drop")
    return jnp.where(fresh[:, None, :, None], value[:, None], moved)


def local(tokens, w_query, w_keyval, w_out, kv_cache, lengths, page_frame, dest_frame):
    seq_index = lax.axis_index("seq")
    seq_count = lax.axis_size("seq")
    tp_index = lax.axis_index("tp")
    tp_count = lax.axis_size("tp")
    req_here, token_count, model_width = tokens.shape
    req_total = req_here * seq_count
    head_dim = kv_cache.shape[3] // 2
    kv_heads = w_keyval.shape[1] // (2 * head_dim)
    query_cols = w_query.shape[1]
    heads_here = query_cols // head_dim
    kv_group = tp_index // (tp_count // kv_heads)
    kv_columns = lax.dynamic_slice_in_dim(w_keyval, kv_group * 2 * head_dim, 2 * head_dim, 1)
    rows = tokens.reshape(-1, model_width)
    query_here = jnp.dot(rows, w_query, preferred_element_type=jnp.float32).astype(jnp.bfloat16)
    keyval_here = jnp.dot(rows, kv_columns, preferred_element_type=jnp.float32).astype(jnp.bfloat16)
    joined = jnp.concatenate([query_here, keyval_here], axis=1).reshape(
        req_here, token_count, query_cols + 2 * head_dim
    )
    frame_store = kv_cache[:, 0]
    frame_total, slot_count, row_width = frame_store.shape
    flat_old = page_frame.reshape(-1)
    flat_new = dest_frame.reshape(-1)
    outgoing = outgoing_pages(frame_store, flat_old, flat_new, seq_index, seq_count)
    own_size = req_here * token_count * (query_cols + 2 * head_dim)
    own_rows = -(-own_size // row_width)
    own_rows = -(-own_rows // 16) * 16
    own_flat = jnp.pad(joined.reshape(own_size), (0, own_rows * row_width - own_size))
    send = jnp.concatenate(
        [
            outgoing,
            jnp.broadcast_to(own_flat.reshape(1, own_rows, row_width), (seq_count, own_rows, row_width)),
        ],
        axis=1,
    )
    received = lax.all_to_all(send, "seq", split_axis=0, concat_axis=0, tiled=True)
    incoming = received[:, :slot_count]
    joined_all = received[:, slot_count:].reshape(seq_count, own_rows * row_width)[:, :own_size].reshape(
        req_total, token_count, query_cols + 2 * head_dim
    )
    queries = joined_all[..., :query_cols].reshape(req_total, token_count, heads_here, head_dim)
    keyval = joined_all[..., query_cols:]

    blocks = page_blocks(frame_store, page_frame, lengths, queries, seq_index)
    arrived = lax.all_to_all(blocks, "seq", split_axis=0, concat_axis=0, tiled=True)
    arrived = arrived.reshape(seq_count, req_here, token_count, heads_here, head_dim + 2)
    src_peak = arrived[..., 0]
    src_total = arrived[..., 1]
    src_partial = arrived[..., 2:]

    own_q = query_here.reshape(req_here, token_count, heads_here, head_dim)
    own_kv = keyval_here.reshape(req_here, token_count, 2 * head_dim)
    token_ids = jnp.arange(token_count, dtype=jnp.int32)
    causal = (token_ids[:, None] >= token_ids[None, :])[None, :, None, :]
    new_scores = jnp.einsum(
        "rtqd,rud->rtqu", own_q, own_kv[..., :head_dim], preferred_element_type=jnp.float32
    ) * head_dim ** (-0.5)
    new_scores = jnp.where(causal, new_scores, LOW_SCORE)
    new_peak = jnp.max(new_scores, axis=-1)
    new_weights = jnp.where(causal, jnp.exp(new_scores - new_peak[..., None]), 0.0).astype(
        jnp.bfloat16
    )
    new_total = jnp.sum(new_weights.astype(jnp.float32), axis=-1)
    new_partial = jnp.einsum(
        "rtqu,rud->rtqd", new_weights, own_kv[..., head_dim:], preferred_element_type=jnp.float32
    )
    top = jnp.maximum(jnp.max(src_peak, axis=0), new_peak)
    src_scale = jnp.exp(src_peak - top[None])
    new_scale = jnp.exp(new_peak - top)
    denominator = jnp.sum(src_scale * src_total, axis=0) + new_scale * new_total
    numerator = jnp.sum(src_scale[..., None] * src_partial, axis=0) + new_scale[..., None] * new_partial
    attended = (numerator / denominator[..., None]).astype(jnp.bfloat16)
    out_term = jnp.dot(
        attended.reshape(req_here * token_count, query_cols),
        w_out,
        preferred_element_type=jnp.float32,
    ).reshape(req_here, token_count, -1)
    col_count = out_term.shape[2] // tp_count
    pieces = out_term.reshape(req_here * token_count, tp_count, col_count).transpose(1, 0, 2)
    gathered = lax.all_to_all(pieces, "tp", split_axis=0, concat_axis=0, tiled=True)
    hidden = jnp.sum(gathered, axis=0).astype(jnp.bfloat16).reshape(req_here, token_count, col_count)

    new_cache = rebuild(
        kv_cache, frame_store, incoming, flat_old, flat_new, lengths, keyval, seq_index, token_count
    )
    return (hidden, new_cache)


def solution(mesh):
    placed = (
        P("seq", None, None),
        P(None, "tp"),
        P(),
        P("tp", None),
        P("seq", "tp", None, None),
        P(),
        P(),
        P(),
    )
    return jax.shard_map(
        local,
        mesh=mesh,
        in_specs=placed,
        out_specs=(P("seq", None, "tp"), P("seq", "tp", None, None)),
        check_vma=False,
    )
```

```python
import jax
import jax.numpy as jnp
from jax import lax
from jax.sharding import PartitionSpec as P

WINDOW = 2048
LOW_SCORE = -1e30
HIGH = lax.Precision.HIGHEST


def page_blocks(store, page_frame, lengths, queries, seq_index):
    frame_total, slot_count, row_width = store.shape
    head_dim = row_width // 2
    req_total, token_count, heads_here, _ = queries.shape
    page_count = page_frame.shape[1]
    flat = page_frame.reshape(-1)
    page_ids = jnp.arange(flat.shape[0], dtype=jnp.int32)
    here = seq_index * frame_total + jnp.arange(frame_total, dtype=jnp.int32)
    matches = flat[None, :] == here[:, None]
    owner = jnp.sum(jnp.where(matches, page_ids[None, :], 0), axis=1)
    occupied = jnp.any(matches, axis=1)
    request = owner // page_count
    page_no = owner % page_count
    length = lengths[request]
    frame_q = queries[request]
    keys_t = jnp.swapaxes(store[..., :head_dim], 1, 2)
    scores = jnp.einsum(
        "fds,fthd->fsth", keys_t, frame_q, preferred_element_type=jnp.float32
    ) * head_dim ** (-0.5)
    token_ids = jnp.arange(token_count, dtype=jnp.int32)
    slot_pos = page_no[:, None] * slot_count + jnp.arange(slot_count, dtype=jnp.int32)[None, :]
    visible = (
        occupied[:, None, None]
        & (slot_pos[:, :, None] < length[:, None, None])
        & (slot_pos[:, :, None] >= (length[:, None] + token_ids[None, :] - WINDOW + 1)[:, None, :])
    )[..., None]
    scores = jnp.where(visible, scores, LOW_SCORE)
    peak = jnp.max(scores, axis=1)
    weights = jnp.where(visible, jnp.exp(scores - peak[:, None]), 0.0).astype(jnp.bfloat16)
    total = jnp.sum(weights.astype(jnp.float32), axis=1)
    partial = jnp.einsum(
        "fsth,fsd->fthd", weights, store[..., head_dim:], preferred_element_type=jnp.float32
    )
    onehot = request[None, :] == jnp.arange(req_total, dtype=jnp.int32)[:, None]
    local_peak = jnp.max(jnp.where(onehot[:, :, None, None], peak[None], LOW_SCORE), axis=1)
    scale = jnp.exp(peak - local_peak[request])
    onehot_f = onehot.astype(jnp.float32)
    local_total = jnp.einsum("rf,fth->rth", onehot_f, scale * total, precision=HIGH)
    local_partial = jnp.einsum("rf,fthd->rthd", onehot_f, scale[..., None] * partial, precision=HIGH)
    return jnp.concatenate(
        [local_peak[..., None], local_total[..., None], local_partial], axis=-1
    )


def outgoing_pages(frame_store, flat_old, flat_new, seq_index, seq_count):
    frame_total = frame_store.shape[0]
    old_device = flat_old // frame_total
    old_local = flat_old % frame_total
    new_device = flat_new // frame_total
    moving = flat_old != flat_new
    peer_ids = jnp.arange(seq_count, dtype=jnp.int32)[:, None]
    leaving = (
        moving[None, :] & (old_device == seq_index)[None, :] & (new_device[None, :] == peer_ids)
    )
    send_local = jnp.sum(jnp.where(leaving, old_local[None, :], 0), axis=1)
    send_any = jnp.any(leaving, axis=1)
    return jnp.where(
        send_any[:, None, None], frame_store[send_local], jnp.zeros_like(frame_store[send_local])
    )


def rebuild(kv_cache, frame_store, incoming, flat_old, flat_new, lengths, keyval, seq_index, token_count):
    frame_total, slot_count, _ = frame_store.shape
    page_count = flat_new.shape[0] // lengths.shape[0]
    page_ids = jnp.arange(flat_new.shape[0], dtype=jnp.int32)
    here = seq_index * frame_total + jnp.arange(frame_total, dtype=jnp.int32)
    matches = flat_new[None, :] == here[:, None]
    owner = jnp.sum(jnp.where(matches, page_ids[None, :], 0), axis=1)
    occupied = jnp.any(matches, axis=1)
    request = owner // page_count
    page_no = owner % page_count
    token_at = (
        page_no[:, None] * slot_count
        + jnp.arange(slot_count, dtype=jnp.int32)[None, :]
        - lengths[request][:, None]
    )
    fresh = occupied[:, None] & (token_at >= 0) & (token_at < token_count)
    rows_new = keyval[request]
    pick = (token_at[..., None] == jnp.arange(token_count, dtype=jnp.int32)).astype(jnp.bfloat16)
    value = jnp.einsum(
        "fjt,ftc->fjc", pick, rows_new, preferred_element_type=jnp.float32
    ).astype(jnp.bfloat16)
    came_from = flat_old[owner]
    arrived = occupied & (came_from != here)
    source = came_from // frame_total
    moved = jnp.where(arrived[:, None, None, None], incoming[source][:, None], kv_cache)
    return jnp.where(fresh[:, None, :, None], value[:, None], moved)


def local(tokens, w_query, w_keyval, w_out, kv_cache, lengths, page_frame, dest_frame):
    seq_index = lax.axis_index("seq")
    seq_count = lax.axis_size("seq")
    tp_index = lax.axis_index("tp")
    tp_count = lax.axis_size("tp")
    req_here, token_count, model_width = tokens.shape
    req_total = req_here * seq_count
    head_dim = kv_cache.shape[3] // 2
    kv_heads = w_keyval.shape[1] // (2 * head_dim)
    query_cols = w_query.shape[1]
    heads_here = query_cols // head_dim
    kv_group = tp_index // (tp_count // kv_heads)
    kv_columns = lax.dynamic_slice_in_dim(w_keyval, kv_group * 2 * head_dim, 2 * head_dim, 1)
    rows = tokens.reshape(-1, model_width)
    query_here = jnp.dot(rows, w_query, preferred_element_type=jnp.float32).astype(jnp.bfloat16)
    keyval_here = jnp.dot(rows, kv_columns, preferred_element_type=jnp.float32).astype(jnp.bfloat16)
    joined = jnp.concatenate([query_here, keyval_here], axis=1).reshape(
        req_here, token_count, query_cols + 2 * head_dim
    )
    frame_store = kv_cache[:, 0]
    frame_total, slot_count, row_width = frame_store.shape
    flat_old = page_frame.reshape(-1)
    flat_new = dest_frame.reshape(-1)
    outgoing = outgoing_pages(frame_store, flat_old, flat_new, seq_index, seq_count)
    own_size = req_here * token_count * (query_cols + 2 * head_dim)
    own_rows = -(-own_size // row_width)
    own_rows = -(-own_rows // 16) * 16
    own_flat = jnp.pad(joined.reshape(own_size), (0, own_rows * row_width - own_size))
    send = jnp.concatenate(
        [
            outgoing,
            jnp.broadcast_to(own_flat.reshape(1, own_rows, row_width), (seq_count, own_rows, row_width)),
        ],
        axis=1,
    )
    received = lax.all_to_all(send, "seq", split_axis=0, concat_axis=0, tiled=True)
    incoming = received[:, :slot_count]
    joined_all = received[:, slot_count:].reshape(seq_count, own_rows * row_width)[:, :own_size].reshape(
        req_total, token_count, query_cols + 2 * head_dim
    )
    queries = joined_all[..., :query_cols].reshape(req_total, token_count, heads_here, head_dim)
    keyval = joined_all[..., query_cols:]

    blocks = page_blocks(frame_store, page_frame, lengths, queries, seq_index)
    arrived = lax.all_to_all(blocks, "seq", split_axis=0, concat_axis=0, tiled=True)
    arrived = arrived.reshape(seq_count, req_here, token_count, heads_here, head_dim + 2)
    src_peak = arrived[..., 0]
    src_total = arrived[..., 1]
    src_partial = arrived[..., 2:]

    own_q = query_here.reshape(req_here, token_count, heads_here, head_dim)
    own_kv = keyval_here.reshape(req_here, token_count, 2 * head_dim)
    token_ids = jnp.arange(token_count, dtype=jnp.int32)
    causal = (token_ids[:, None] >= token_ids[None, :])[None, :, None, :]
    new_scores = jnp.einsum(
        "rtqd,rud->rtqu", own_q, own_kv[..., :head_dim], preferred_element_type=jnp.float32
    ) * head_dim ** (-0.5)
    new_scores = jnp.where(causal, new_scores, LOW_SCORE)
    new_peak = jnp.max(new_scores, axis=-1)
    new_weights = jnp.where(causal, jnp.exp(new_scores - new_peak[..., None]), 0.0).astype(
        jnp.bfloat16
    )
    new_total = jnp.sum(new_weights.astype(jnp.float32), axis=-1)
    new_partial = jnp.einsum(
        "rtqu,rud->rtqd", new_weights, own_kv[..., head_dim:], preferred_element_type=jnp.float32
    )
    top = jnp.maximum(jnp.max(src_peak, axis=0), new_peak)
    src_scale = jnp.exp(src_peak - top[None])
    new_scale = jnp.exp(new_peak - top)
    denominator = jnp.sum(src_scale * src_total, axis=0) + new_scale * new_total
    numerator = jnp.sum(src_scale[..., None] * src_partial, axis=0) + new_scale[..., None] * new_partial
    attended = (numerator / denominator[..., None]).astype(jnp.bfloat16)
    out_term = jnp.dot(
        attended.reshape(req_here * token_count, query_cols),
        w_out,
        preferred_element_type=jnp.float32,
    ).reshape(req_here, token_count, -1)
    col_count = out_term.shape[2] // tp_count
    pieces = out_term.reshape(req_here * token_count, tp_count, col_count).transpose(1, 0, 2)
    gathered = lax.all_to_all(pieces, "tp", split_axis=0, concat_axis=0, tiled=True)
    hidden = jnp.sum(gathered, axis=0).astype(jnp.bfloat16).reshape(req_here, token_count, col_count)

    new_cache = rebuild(
        kv_cache, frame_store, incoming, flat_old, flat_new, lengths, keyval, seq_index, token_count
    )
    return (hidden, new_cache)


def solution(mesh):
    placed = (
        P("seq", None, None),
        P(None, "tp"),
        P(),
        P("tp", None),
        P("seq", "tp", None, None),
        P(),
        P(),
        P(),
    )
    return jax.shard_map(
        local,
        mesh=mesh,
        in_specs=placed,
        out_specs=(P("seq", None, "tp"), P("seq", "tp", None, None)),
        check_vma=False,
    )
```

```python
import jax
import jax.numpy as jnp
from jax import lax
from jax.sharding import PartitionSpec as P

WINDOW = 2048
LOW_SCORE = -1e30
HIGH = lax.Precision.HIGH


def page_blocks(store, page_frame, lengths, queries, seq_index):
    frame_total, slot_count, row_width = store.shape
    head_dim = row_width // 2
    req_total, token_count, heads_here, _ = queries.shape
    page_count = page_frame.shape[1]
    flat = page_frame.reshape(-1)
    page_ids = jnp.arange(flat.shape[0], dtype=jnp.int32)
    here = seq_index * frame_total + jnp.arange(frame_total, dtype=jnp.int32)
    matches = flat[None, :] == here[:, None]
    owner = jnp.sum(jnp.where(matches, page_ids[None, :], 0), axis=1)
    occupied = jnp.any(matches, axis=1)
    request = owner // page_count
    page_no = owner % page_count
    length = lengths[request]
    frame_q = queries[request]
    keys_t = jnp.swapaxes(store[..., :head_dim], 1, 2)
    scores = jnp.einsum(
        "fds,fthd->fsth", keys_t, frame_q, preferred_element_type=jnp.float32
    ) * head_dim ** (-0.5)
    token_ids = jnp.arange(token_count, dtype=jnp.int32)
    slot_pos = page_no[:, None] * slot_count + jnp.arange(slot_count, dtype=jnp.int32)[None, :]
    visible = (
        occupied[:, None, None]
        & (slot_pos[:, :, None] < length[:, None, None])
        & (slot_pos[:, :, None] >= (length[:, None] + token_ids[None, :] - WINDOW + 1)[:, None, :])
    )[..., None]
    scores = jnp.where(visible, scores, LOW_SCORE)
    peak = jnp.max(scores, axis=1)
    weights = jnp.where(visible, jnp.exp(scores - peak[:, None]), 0.0).astype(jnp.bfloat16)
    total = jnp.sum(weights.astype(jnp.float32), axis=1)
    partial = jnp.einsum(
        "fsth,fsd->fthd", weights, store[..., head_dim:], preferred_element_type=jnp.float32
    )
    onehot = request[None, :] == jnp.arange(req_total, dtype=jnp.int32)[:, None]
    local_peak = jnp.max(jnp.where(onehot[:, :, None, None], peak[None], LOW_SCORE), axis=1)
    scale = jnp.exp(peak - local_peak[request])
    onehot_f = onehot.astype(jnp.float32)
    local_total = jnp.einsum("rf,fth->rth", onehot_f, scale * total, precision=HIGH)
    local_partial = jnp.einsum("rf,fthd->rthd", onehot_f, scale[..., None] * partial, precision=HIGH)
    return jnp.concatenate(
        [local_peak[..., None], local_total[..., None], local_partial], axis=-1
    )


def outgoing_pages(frame_store, flat_old, flat_new, seq_index, seq_count):
    frame_total = frame_store.shape[0]
    old_device = flat_old // frame_total
    old_local = flat_old % frame_total
    new_device = flat_new // frame_total
    moving = flat_old != flat_new
    peer_ids = jnp.arange(seq_count, dtype=jnp.int32)[:, None]
    leaving = (
        moving[None, :] & (old_device == seq_index)[None, :] & (new_device[None, :] == peer_ids)
    )
    send_local = jnp.sum(jnp.where(leaving, old_local[None, :], 0), axis=1)
    send_any = jnp.any(leaving, axis=1)
    return jnp.where(
        send_any[:, None, None], frame_store[send_local], jnp.zeros_like(frame_store[send_local])
    )


def rebuild(kv_cache, frame_store, incoming, flat_old, flat_new, lengths, keyval, seq_index, token_count):
    frame_total, slot_count, _ = frame_store.shape
    page_count = flat_new.shape[0] // lengths.shape[0]
    page_ids = jnp.arange(flat_new.shape[0], dtype=jnp.int32)
    here = seq_index * frame_total + jnp.arange(frame_total, dtype=jnp.int32)
    matches = flat_new[None, :] == here[:, None]
    owner = jnp.sum(jnp.where(matches, page_ids[None, :], 0), axis=1)
    occupied = jnp.any(matches, axis=1)
    request = owner // page_count
    page_no = owner % page_count
    token_at = (
        page_no[:, None] * slot_count
        + jnp.arange(slot_count, dtype=jnp.int32)[None, :]
        - lengths[request][:, None]
    )
    fresh = occupied[:, None] & (token_at >= 0) & (token_at < token_count)
    rows_new = keyval[request]
    pick = (token_at[..., None] == jnp.arange(token_count, dtype=jnp.int32)).astype(jnp.bfloat16)
    value = jnp.einsum(
        "fjt,ftc->fjc", pick, rows_new, preferred_element_type=jnp.float32
    ).astype(jnp.bfloat16)
    came_from = flat_old[owner]
    arrived = occupied & (came_from != here)
    source = came_from // frame_total
    moved = jnp.where(arrived[:, None, None, None], incoming[source][:, None], kv_cache)
    return jnp.where(fresh[:, None, :, None], value[:, None], moved)


def local(tokens, w_query, w_keyval, w_out, kv_cache, lengths, page_frame, dest_frame):
    seq_index = lax.axis_index("seq")
    seq_count = lax.axis_size("seq")
    tp_index = lax.axis_index("tp")
    tp_count = lax.axis_size("tp")
    req_here, token_count, model_width = tokens.shape
    req_total = req_here * seq_count
    head_dim = kv_cache.shape[3] // 2
    kv_heads = w_keyval.shape[1] // (2 * head_dim)
    query_cols = w_query.shape[1]
    heads_here = query_cols // head_dim
    kv_group = tp_index // (tp_count // kv_heads)
    kv_columns = lax.dynamic_slice_in_dim(w_keyval, kv_group * 2 * head_dim, 2 * head_dim, 1)
    rows = tokens.reshape(-1, model_width)
    query_here = jnp.dot(rows, w_query, preferred_element_type=jnp.float32).astype(jnp.bfloat16)
    keyval_here = jnp.dot(rows, kv_columns, preferred_element_type=jnp.float32).astype(jnp.bfloat16)
    joined = jnp.concatenate([query_here, keyval_here], axis=1).reshape(
        req_here, token_count, query_cols + 2 * head_dim
    )
    frame_store = kv_cache[:, 0]
    frame_total, slot_count, row_width = frame_store.shape
    flat_old = page_frame.reshape(-1)
    flat_new = dest_frame.reshape(-1)
    outgoing = outgoing_pages(frame_store, flat_old, flat_new, seq_index, seq_count)
    own_size = req_here * token_count * (query_cols + 2 * head_dim)
    own_rows = -(-own_size // row_width)
    own_rows = -(-own_rows // 16) * 16
    own_flat = jnp.pad(joined.reshape(own_size), (0, own_rows * row_width - own_size))
    send = jnp.concatenate(
        [
            outgoing,
            jnp.broadcast_to(own_flat.reshape(1, own_rows, row_width), (seq_count, own_rows, row_width)),
        ],
        axis=1,
    )
    received = lax.all_to_all(send, "seq", split_axis=0, concat_axis=0, tiled=True)
    incoming = received[:, :slot_count]
    joined_all = received[:, slot_count:].reshape(seq_count, own_rows * row_width)[:, :own_size].reshape(
        req_total, token_count, query_cols + 2 * head_dim
    )
    queries = joined_all[..., :query_cols].reshape(req_total, token_count, heads_here, head_dim)
    keyval = joined_all[..., query_cols:]

    blocks = page_blocks(frame_store, page_frame, lengths, queries, seq_index)
    arrived = lax.all_to_all(blocks, "seq", split_axis=0, concat_axis=0, tiled=True)
    arrived = arrived.reshape(seq_count, req_here, token_count, heads_here, head_dim + 2)
    src_peak = arrived[..., 0]
    src_total = arrived[..., 1]
    src_partial = arrived[..., 2:]

    own_q = query_here.reshape(req_here, token_count, heads_here, head_dim)
    own_kv = keyval_here.reshape(req_here, token_count, 2 * head_dim)
    token_ids = jnp.arange(token_count, dtype=jnp.int32)
    causal = (token_ids[:, None] >= token_ids[None, :])[None, :, None, :]
    new_scores = jnp.einsum(
        "rtqd,rud->rtqu", own_q, own_kv[..., :head_dim], preferred_element_type=jnp.float32
    ) * head_dim ** (-0.5)
    new_scores = jnp.where(causal, new_scores, LOW_SCORE)
    new_peak = jnp.max(new_scores, axis=-1)
    new_weights = jnp.where(causal, jnp.exp(new_scores - new_peak[..., None]), 0.0).astype(
        jnp.bfloat16
    )
    new_total = jnp.sum(new_weights.astype(jnp.float32), axis=-1)
    new_partial = jnp.einsum(
        "rtqu,rud->rtqd", new_weights, own_kv[..., head_dim:], preferred_element_type=jnp.float32
    )
    top = jnp.maximum(jnp.max(src_peak, axis=0), new_peak)
    src_scale = jnp.exp(src_peak - top[None])
    new_scale = jnp.exp(new_peak - top)
    denominator = jnp.sum(src_scale * src_total, axis=0) + new_scale * new_total
    numerator = jnp.sum(src_scale[..., None] * src_partial, axis=0) + new_scale[..., None] * new_partial
    attended = (numerator / denominator[..., None]).astype(jnp.bfloat16)
    out_term = jnp.dot(
        attended.reshape(req_here * token_count, query_cols),
        w_out,
        preferred_element_type=jnp.float32,
    ).reshape(req_here, token_count, -1)
    col_count = out_term.shape[2] // tp_count
    pieces = out_term.reshape(req_here * token_count, tp_count, col_count).transpose(1, 0, 2)
    gathered = lax.all_to_all(pieces, "tp", split_axis=0, concat_axis=0, tiled=True)
    hidden = jnp.sum(gathered, axis=0).astype(jnp.bfloat16).reshape(req_here, token_count, col_count)

    new_cache = rebuild(
        kv_cache, frame_store, incoming, flat_old, flat_new, lengths, keyval, seq_index, token_count
    )
    return (hidden, new_cache)


def solution(mesh):
    placed = (
        P("seq", None, None),
        P(None, "tp"),
        P(),
        P("tp", None),
        P("seq", "tp", None, None),
        P(),
        P(),
        P(),
    )
    return jax.shard_map(
        local,
        mesh=mesh,
        in_specs=placed,
        out_specs=(P("seq", None, "tp"), P("seq", "tp", None, None)),
        check_vma=False,
    )
```

```python
import jax
import jax.numpy as jnp
from jax import lax
from jax.sharding import PartitionSpec as P
from jax.experimental import pallas as pl
from jax.experimental.pallas import tpu as pltpu

WINDOW = 2048
LOW_SCORE = -1e30
HIGH = lax.Precision.HIGH


FRAMES_PER_STEP = 16


def frame_kernel(store_ref, q_ref, lower_ref, upper_ref, peak_ref, total_ref, partial_ref):
    head_dim = q_ref.shape[2]
    slot_count = store_ref.shape[1]
    for b in range(store_ref.shape[0]):
        page = store_ref[b]
        keys = page[:, :head_dim]
        values = page[:, head_dim:]
        scores = lax.dot_general(
            q_ref[b], keys, (((1,), (1,)), ((), ())), preferred_element_type=jnp.float32
        ) * head_dim ** (-0.5)
        slot = lax.broadcasted_iota(jnp.int32, scores.shape, 1)
        visible = (slot >= lower_ref[b]) & (slot < upper_ref[b])
        scores = jnp.where(visible, scores, LOW_SCORE)
        peak = jnp.max(scores, axis=1, keepdims=True)
        weights = jnp.where(visible, jnp.exp(scores - peak), 0.0).astype(jnp.bfloat16)
        peak_ref[b] = peak
        total_ref[b] = jnp.sum(weights.astype(jnp.float32), axis=1, keepdims=True)
        partial_ref[b] = jnp.dot(weights, values, preferred_element_type=jnp.float32)


def frame_attention(store, frame_q, lower, upper):
    frame_total, slot_count, row_width = store.shape
    rows, head_dim = frame_q.shape[1], frame_q.shape[2]
    step = FRAMES_PER_STEP if frame_total % FRAMES_PER_STEP == 0 else 1
    return pl.pallas_call(
        frame_kernel,
        grid=(frame_total // step,),
        in_specs=[
            pl.BlockSpec((step, slot_count, row_width), lambda i: (i, 0, 0)),
            pl.BlockSpec((step, rows, head_dim), lambda i: (i, 0, 0)),
            pl.BlockSpec((step, rows, 1), lambda i: (i, 0, 0)),
            pl.BlockSpec((step, rows, 1), lambda i: (i, 0, 0)),
        ],
        out_specs=[
            pl.BlockSpec((step, rows, 1), lambda i: (i, 0, 0)),
            pl.BlockSpec((step, rows, 1), lambda i: (i, 0, 0)),
            pl.BlockSpec((step, rows, head_dim), lambda i: (i, 0, 0)),
        ],
        out_shape=[
            jax.ShapeDtypeStruct((frame_total, rows, 1), jnp.float32),
            jax.ShapeDtypeStruct((frame_total, rows, 1), jnp.float32),
            jax.ShapeDtypeStruct((frame_total, rows, head_dim), jnp.float32),
        ],
        cost_estimate=pl.CostEstimate(
            flops=4 * frame_total * rows * slot_count * head_dim,
            transcendentals=frame_total * rows * slot_count,
            bytes_accessed=store.size * 2 + frame_total * rows * (head_dim * 6 + 16),
        ),
    )(store, frame_q, lower, upper)


def page_blocks(store, page_frame, lengths, queries, seq_index):
    frame_total, slot_count, row_width = store.shape
    head_dim = row_width // 2
    req_total, token_count, heads_here, _ = queries.shape
    page_count = page_frame.shape[1]
    flat = page_frame.reshape(-1)
    page_ids = jnp.arange(flat.shape[0], dtype=jnp.int32)
    here = seq_index * frame_total + jnp.arange(frame_total, dtype=jnp.int32)
    matches = flat[None, :] == here[:, None]
    owner = jnp.sum(jnp.where(matches, page_ids[None, :], 0), axis=1)
    occupied = jnp.any(matches, axis=1)
    request = owner // page_count
    page_no = owner % page_count
    length = lengths[request]
    frame_q = queries[request]
    token_ids = jnp.arange(token_count, dtype=jnp.int32)
    base = page_no * slot_count
    upper = jnp.where(occupied, length - base, 0)
    lower = length[:, None] + token_ids[None, :] - WINDOW + 1 - base[:, None]
    rows_per_frame = token_count * heads_here
    lower = jnp.repeat(lower, heads_here, axis=1).reshape(frame_total, rows_per_frame, 1)
    upper = jnp.broadcast_to(upper[:, None, None], (frame_total, rows_per_frame, 1))
    peak, total, partial = frame_attention(
        store, frame_q.reshape(frame_total, rows_per_frame, head_dim), lower, upper
    )
    peak = peak.reshape(frame_total, token_count, heads_here)
    total = total.reshape(frame_total, token_count, heads_here)
    partial = partial.reshape(frame_total, token_count, heads_here, head_dim)
    onehot = request[None, :] == jnp.arange(req_total, dtype=jnp.int32)[:, None]
    local_peak = jnp.max(jnp.where(onehot[:, :, None, None], peak[None], LOW_SCORE), axis=1)
    scale = jnp.exp(peak - local_peak[request])
    onehot_f = onehot.astype(jnp.float32)
    local_total = jnp.einsum("rf,fth->rth", onehot_f, scale * total, precision=HIGH)
    local_partial = jnp.einsum("rf,fthd->rthd", onehot_f, scale[..., None] * partial, precision=HIGH)
    return jnp.concatenate(
        [local_peak[..., None], local_total[..., None], local_partial], axis=-1
    )


def outgoing_pages(frame_store, flat_old, flat_new, seq_index, seq_count):
    frame_total = frame_store.shape[0]
    old_device = flat_old // frame_total
    old_local = flat_old % frame_total
    new_device = flat_new // frame_total
    moving = flat_old != flat_new
    peer_ids = jnp.arange(seq_count, dtype=jnp.int32)[:, None]
    leaving = (
        moving[None, :] & (old_device == seq_index)[None, :] & (new_device[None, :] == peer_ids)
    )
    send_local = jnp.sum(jnp.where(leaving, old_local[None, :], 0), axis=1)
    send_any = jnp.any(leaving, axis=1)
    return jnp.where(
        send_any[:, None, None], frame_store[send_local], jnp.zeros_like(frame_store[send_local])
    )


def rebuild(kv_cache, frame_store, incoming, flat_old, flat_new, lengths, keyval, seq_index, token_count):
    frame_total, slot_count, _ = frame_store.shape
    page_count = flat_new.shape[0] // lengths.shape[0]
    page_ids = jnp.arange(flat_new.shape[0], dtype=jnp.int32)
    here = seq_index * frame_total + jnp.arange(frame_total, dtype=jnp.int32)
    matches = flat_new[None, :] == here[:, None]
    owner = jnp.sum(jnp.where(matches, page_ids[None, :], 0), axis=1)
    occupied = jnp.any(matches, axis=1)
    request = owner // page_count
    page_no = owner % page_count
    token_at = (
        page_no[:, None] * slot_count
        + jnp.arange(slot_count, dtype=jnp.int32)[None, :]
        - lengths[request][:, None]
    )
    fresh = occupied[:, None] & (token_at >= 0) & (token_at < token_count)
    rows_new = keyval[request]
    pick = (token_at[..., None] == jnp.arange(token_count, dtype=jnp.int32)).astype(jnp.bfloat16)
    value = jnp.einsum(
        "fjt,ftc->fjc", pick, rows_new, preferred_element_type=jnp.float32
    ).astype(jnp.bfloat16)
    came_from = flat_old[owner]
    arrived = occupied & (came_from != here)
    source = came_from // frame_total
    moved = jnp.where(arrived[:, None, None, None], incoming[source][:, None], kv_cache)
    return jnp.where(fresh[:, None, :, None], value[:, None], moved)


def local(tokens, w_query, w_keyval, w_out, kv_cache, lengths, page_frame, dest_frame):
    seq_index = lax.axis_index("seq")
    seq_count = lax.axis_size("seq")
    tp_index = lax.axis_index("tp")
    tp_count = lax.axis_size("tp")
    req_here, token_count, model_width = tokens.shape
    req_total = req_here * seq_count
    head_dim = kv_cache.shape[3] // 2
    kv_heads = w_keyval.shape[1] // (2 * head_dim)
    query_cols = w_query.shape[1]
    heads_here = query_cols // head_dim
    kv_group = tp_index // (tp_count // kv_heads)
    kv_columns = lax.dynamic_slice_in_dim(w_keyval, kv_group * 2 * head_dim, 2 * head_dim, 1)
    rows = tokens.reshape(-1, model_width)
    query_here = jnp.dot(rows, w_query, preferred_element_type=jnp.float32).astype(jnp.bfloat16)
    keyval_here = jnp.dot(rows, kv_columns, preferred_element_type=jnp.float32).astype(jnp.bfloat16)
    joined = jnp.concatenate([query_here, keyval_here], axis=1).reshape(
        req_here, token_count, query_cols + 2 * head_dim
    )
    frame_store = kv_cache[:, 0]
    frame_total, slot_count, row_width = frame_store.shape
    flat_old = page_frame.reshape(-1)
    flat_new = dest_frame.reshape(-1)
    outgoing = outgoing_pages(frame_store, flat_old, flat_new, seq_index, seq_count)
    own_size = req_here * token_count * (query_cols + 2 * head_dim)
    own_rows = -(-own_size // row_width)
    own_rows = -(-own_rows // 16) * 16
    own_flat = jnp.pad(joined.reshape(own_size), (0, own_rows * row_width - own_size))
    send = jnp.concatenate(
        [
            outgoing,
            jnp.broadcast_to(own_flat.reshape(1, own_rows, row_width), (seq_count, own_rows, row_width)),
        ],
        axis=1,
    )
    received = lax.all_to_all(send, "seq", split_axis=0, concat_axis=0, tiled=True)
    incoming = received[:, :slot_count]
    joined_all = received[:, slot_count:].reshape(seq_count, own_rows * row_width)[:, :own_size].reshape(
        req_total, token_count, query_cols + 2 * head_dim
    )
    queries = joined_all[..., :query_cols].reshape(req_total, token_count, heads_here, head_dim)
    keyval = joined_all[..., query_cols:]

    blocks = page_blocks(frame_store, page_frame, lengths, queries, seq_index)
    arrived = lax.all_to_all(blocks, "seq", split_axis=0, concat_axis=0, tiled=True)
    arrived = arrived.reshape(seq_count, req_here, token_count, heads_here, head_dim + 2)
    src_peak = arrived[..., 0]
    src_total = arrived[..., 1]
    src_partial = arrived[..., 2:]

    own_q = query_here.reshape(req_here, token_count, heads_here, head_dim)
    own_kv = keyval_here.reshape(req_here, token_count, 2 * head_dim)
    token_ids = jnp.arange(token_count, dtype=jnp.int32)
    causal = (token_ids[:, None] >= token_ids[None, :])[None, :, None, :]
    new_scores = jnp.einsum(
        "rtqd,rud->rtqu", own_q, own_kv[..., :head_dim], preferred_element_type=jnp.float32
    ) * head_dim ** (-0.5)
    new_scores = jnp.where(causal, new_scores, LOW_SCORE)
    new_peak = jnp.max(new_scores, axis=-1)
    new_weights = jnp.where(causal, jnp.exp(new_scores - new_peak[..., None]), 0.0).astype(
        jnp.bfloat16
    )
    new_total = jnp.sum(new_weights.astype(jnp.float32), axis=-1)
    new_partial = jnp.einsum(
        "rtqu,rud->rtqd", new_weights, own_kv[..., head_dim:], preferred_element_type=jnp.float32
    )
    top = jnp.maximum(jnp.max(src_peak, axis=0), new_peak)
    src_scale = jnp.exp(src_peak - top[None])
    new_scale = jnp.exp(new_peak - top)
    denominator = jnp.sum(src_scale * src_total, axis=0) + new_scale * new_total
    numerator = jnp.sum(src_scale[..., None] * src_partial, axis=0) + new_scale[..., None] * new_partial
    attended = (numerator / denominator[..., None]).astype(jnp.bfloat16)
    out_term = jnp.dot(
        attended.reshape(req_here * token_count, query_cols),
        w_out,
        preferred_element_type=jnp.float32,
    ).reshape(req_here, token_count, -1)
    col_count = out_term.shape[2] // tp_count
    pieces = out_term.reshape(req_here * token_count, tp_count, col_count).transpose(1, 0, 2)
    gathered = lax.all_to_all(pieces, "tp", split_axis=0, concat_axis=0, tiled=True)
    hidden = jnp.sum(gathered, axis=0).astype(jnp.bfloat16).reshape(req_here, token_count, col_count)

    new_cache = rebuild(
        kv_cache, frame_store, incoming, flat_old, flat_new, lengths, keyval, seq_index, token_count
    )
    return (hidden, new_cache)


def solution(mesh):
    placed = (
        P("seq", None, None),
        P(None, "tp"),
        P(),
        P("tp", None),
        P("seq", "tp", None, None),
        P(),
        P(),
        P(),
    )
    return jax.shard_map(
        local,
        mesh=mesh,
        in_specs=placed,
        out_specs=(P("seq", None, "tp"), P("seq", "tp", None, None)),
        check_vma=False,
    )
```

```python
import jax
import jax.numpy as jnp
from jax import lax
from jax.sharding import PartitionSpec as P
from jax.experimental import pallas as pl
from jax.experimental.pallas import tpu as pltpu

WINDOW = 2048
LOW_SCORE = -1e30
HIGH = lax.Precision.HIGH


FRAMES_PER_STEP = 16


def frame_kernel(store_ref, q_ref, lower_ref, upper_ref, out_ref):
    head_dim = q_ref.shape[2] // 2
    page = store_ref[...]
    scores = jnp.einsum(
        "bqc,bkc->bqk", q_ref[...], page, preferred_element_type=jnp.float32
    ) * head_dim ** (-0.5)
    slot = lax.broadcasted_iota(jnp.int32, scores.shape, 2)
    visible = (slot >= lower_ref[...]) & (slot < upper_ref[...])
    scores = jnp.where(visible, scores, LOW_SCORE)
    peak = jnp.max(scores, axis=2, keepdims=True)
    weights = jnp.where(visible, jnp.exp(scores - peak), 0.0).astype(jnp.bfloat16)
    total = jnp.sum(weights.astype(jnp.float32), axis=2, keepdims=True)
    mixed = jnp.einsum("bqk,bkc->bqc", weights, page, preferred_element_type=jnp.float32)
    lane = lax.broadcasted_iota(jnp.int32, mixed.shape, 2)
    out_ref[...] = jnp.where(lane == 0, peak, jnp.where(lane == 1, total, mixed))


def frame_attention(store, frame_q, lower, upper):
    frame_total, slot_count, row_width = store.shape
    rows, head_dim = frame_q.shape[1], frame_q.shape[2]
    padded_q = jnp.concatenate([frame_q, jnp.zeros_like(frame_q)], axis=2)
    step = FRAMES_PER_STEP if frame_total % FRAMES_PER_STEP == 0 else 1
    packed = pl.pallas_call(
        frame_kernel,
        grid=(frame_total // step,),
        in_specs=[
            pl.BlockSpec((step, slot_count, row_width), lambda i: (i, 0, 0)),
            pl.BlockSpec((step, rows, row_width), lambda i: (i, 0, 0)),
            pl.BlockSpec((step, rows, 1), lambda i: (i, 0, 0)),
            pl.BlockSpec((step, rows, 1), lambda i: (i, 0, 0)),
        ],
        out_specs=pl.BlockSpec((step, rows, row_width), lambda i: (i, 0, 0)),
        out_shape=jax.ShapeDtypeStruct((frame_total, rows, row_width), jnp.float32),
        cost_estimate=pl.CostEstimate(
            flops=4 * frame_total * rows * slot_count * row_width,
            transcendentals=frame_total * rows * slot_count,
            bytes_accessed=store.size * 2 + frame_total * rows * (row_width * 6 + 8),
        ),
    )(store, padded_q, lower, upper)
    return packed[..., 0], packed[..., 1], packed[..., head_dim:]


def page_blocks(store, page_frame, lengths, queries, seq_index):
    frame_total, slot_count, row_width = store.shape
    head_dim = row_width // 2
    req_total, token_count, heads_here, _ = queries.shape
    page_count = page_frame.shape[1]
    flat = page_frame.reshape(-1)
    page_ids = jnp.arange(flat.shape[0], dtype=jnp.int32)
    here = seq_index * frame_total + jnp.arange(frame_total, dtype=jnp.int32)
    matches = flat[None, :] == here[:, None]
    owner = jnp.sum(jnp.where(matches, page_ids[None, :], 0), axis=1)
    occupied = jnp.any(matches, axis=1)
    request = owner // page_count
    page_no = owner % page_count
    length = lengths[request]
    frame_q = queries[request]
    token_ids = jnp.arange(token_count, dtype=jnp.int32)
    base = page_no * slot_count
    upper = jnp.where(occupied, length - base, 0)
    lower = length[:, None] + token_ids[None, :] - WINDOW + 1 - base[:, None]
    rows_per_frame = token_count * heads_here
    lower = jnp.repeat(lower, heads_here, axis=1).reshape(frame_total, rows_per_frame, 1)
    upper = jnp.broadcast_to(upper[:, None, None], (frame_total, rows_per_frame, 1))
    peak, total, partial = frame_attention(
        store, frame_q.reshape(frame_total, rows_per_frame, head_dim), lower, upper
    )
    peak = peak.reshape(frame_total, token_count, heads_here)
    total = total.reshape(frame_total, token_count, heads_here)
    partial = partial.reshape(frame_total, token_count, heads_here, head_dim)
    onehot = request[None, :] == jnp.arange(req_total, dtype=jnp.int32)[:, None]
    local_peak = jnp.max(jnp.where(onehot[:, :, None, None], peak[None], LOW_SCORE), axis=1)
    scale = jnp.exp(peak - local_peak[request])
    onehot_f = onehot.astype(jnp.float32)
    local_total = jnp.einsum("rf,fth->rth", onehot_f, scale * total, precision=HIGH)
    local_partial = jnp.einsum("rf,fthd->rthd", onehot_f, scale[..., None] * partial, precision=HIGH)
    return jnp.concatenate(
        [local_peak[..., None], local_total[..., None], local_partial], axis=-1
    )


def outgoing_pages(frame_store, flat_old, flat_new, seq_index, seq_count):
    frame_total = frame_store.shape[0]
    old_device = flat_old // frame_total
    old_local = flat_old % frame_total
    new_device = flat_new // frame_total
    moving = flat_old != flat_new
    peer_ids = jnp.arange(seq_count, dtype=jnp.int32)[:, None]
    leaving = (
        moving[None, :] & (old_device == seq_index)[None, :] & (new_device[None, :] == peer_ids)
    )
    send_local = jnp.sum(jnp.where(leaving, old_local[None, :], 0), axis=1)
    send_any = jnp.any(leaving, axis=1)
    return jnp.where(
        send_any[:, None, None], frame_store[send_local], jnp.zeros_like(frame_store[send_local])
    )


def rebuild(kv_cache, frame_store, incoming, flat_old, flat_new, lengths, keyval, seq_index, token_count):
    frame_total, slot_count, _ = frame_store.shape
    page_count = flat_new.shape[0] // lengths.shape[0]
    page_ids = jnp.arange(flat_new.shape[0], dtype=jnp.int32)
    here = seq_index * frame_total + jnp.arange(frame_total, dtype=jnp.int32)
    matches = flat_new[None, :] == here[:, None]
    owner = jnp.sum(jnp.where(matches, page_ids[None, :], 0), axis=1)
    occupied = jnp.any(matches, axis=1)
    request = owner // page_count
    page_no = owner % page_count
    token_at = (
        page_no[:, None] * slot_count
        + jnp.arange(slot_count, dtype=jnp.int32)[None, :]
        - lengths[request][:, None]
    )
    fresh = occupied[:, None] & (token_at >= 0) & (token_at < token_count)
    rows_new = keyval[request]
    pick = (token_at[..., None] == jnp.arange(token_count, dtype=jnp.int32)).astype(jnp.bfloat16)
    value = jnp.einsum(
        "fjt,ftc->fjc", pick, rows_new, preferred_element_type=jnp.float32
    ).astype(jnp.bfloat16)
    came_from = flat_old[owner]
    arrived = occupied & (came_from != here)
    source = came_from // frame_total
    moved = jnp.where(arrived[:, None, None, None], incoming[source][:, None], kv_cache)
    return jnp.where(fresh[:, None, :, None], value[:, None], moved)


def local(tokens, w_query, w_keyval, w_out, kv_cache, lengths, page_frame, dest_frame):
    seq_index = lax.axis_index("seq")
    seq_count = lax.axis_size("seq")
    tp_index = lax.axis_index("tp")
    tp_count = lax.axis_size("tp")
    req_here, token_count, model_width = tokens.shape
    req_total = req_here * seq_count
    head_dim = kv_cache.shape[3] // 2
    kv_heads = w_keyval.shape[1] // (2 * head_dim)
    query_cols = w_query.shape[1]
    heads_here = query_cols // head_dim
    kv_group = tp_index // (tp_count // kv_heads)
    kv_columns = lax.dynamic_slice_in_dim(w_keyval, kv_group * 2 * head_dim, 2 * head_dim, 1)
    rows = tokens.reshape(-1, model_width)
    query_here = jnp.dot(rows, w_query, preferred_element_type=jnp.float32).astype(jnp.bfloat16)
    keyval_here = jnp.dot(rows, kv_columns, preferred_element_type=jnp.float32).astype(jnp.bfloat16)
    joined = jnp.concatenate([query_here, keyval_here], axis=1).reshape(
        req_here, token_count, query_cols + 2 * head_dim
    )
    frame_store = kv_cache[:, 0]
    frame_total, slot_count, row_width = frame_store.shape
    flat_old = page_frame.reshape(-1)
    flat_new = dest_frame.reshape(-1)
    outgoing = outgoing_pages(frame_store, flat_old, flat_new, seq_index, seq_count)
    own_size = req_here * token_count * (query_cols + 2 * head_dim)
    own_rows = -(-own_size // row_width)
    own_rows = -(-own_rows // 16) * 16
    own_flat = jnp.pad(joined.reshape(own_size), (0, own_rows * row_width - own_size))
    send = jnp.concatenate(
        [
            outgoing,
            jnp.broadcast_to(own_flat.reshape(1, own_rows, row_width), (seq_count, own_rows, row_width)),
        ],
        axis=1,
    )
    received = lax.all_to_all(send, "seq", split_axis=0, concat_axis=0, tiled=True)
    incoming = received[:, :slot_count]
    joined_all = received[:, slot_count:].reshape(seq_count, own_rows * row_width)[:, :own_size].reshape(
        req_total, token_count, query_cols + 2 * head_dim
    )
    queries = joined_all[..., :query_cols].reshape(req_total, token_count, heads_here, head_dim)
    keyval = joined_all[..., query_cols:]

    blocks = page_blocks(frame_store, page_frame, lengths, queries, seq_index)
    arrived = lax.all_to_all(blocks, "seq", split_axis=0, concat_axis=0, tiled=True)
    arrived = arrived.reshape(seq_count, req_here, token_count, heads_here, head_dim + 2)
    src_peak = arrived[..., 0]
    src_total = arrived[..., 1]
    src_partial = arrived[..., 2:]

    own_q = query_here.reshape(req_here, token_count, heads_here, head_dim)
    own_kv = keyval_here.reshape(req_here, token_count, 2 * head_dim)
    token_ids = jnp.arange(token_count, dtype=jnp.int32)
    causal = (token_ids[:, None] >= token_ids[None, :])[None, :, None, :]
    new_scores = jnp.einsum(
        "rtqd,rud->rtqu", own_q, own_kv[..., :head_dim], preferred_element_type=jnp.float32
    ) * head_dim ** (-0.5)
    new_scores = jnp.where(causal, new_scores, LOW_SCORE)
    new_peak = jnp.max(new_scores, axis=-1)
    new_weights = jnp.where(causal, jnp.exp(new_scores - new_peak[..., None]), 0.0).astype(
        jnp.bfloat16
    )
    new_total = jnp.sum(new_weights.astype(jnp.float32), axis=-1)
    new_partial = jnp.einsum(
        "rtqu,rud->rtqd", new_weights, own_kv[..., head_dim:], preferred_element_type=jnp.float32
    )
    top = jnp.maximum(jnp.max(src_peak, axis=0), new_peak)
    src_scale = jnp.exp(src_peak - top[None])
    new_scale = jnp.exp(new_peak - top)
    denominator = jnp.sum(src_scale * src_total, axis=0) + new_scale * new_total
    numerator = jnp.sum(src_scale[..., None] * src_partial, axis=0) + new_scale[..., None] * new_partial
    attended = (numerator / denominator[..., None]).astype(jnp.bfloat16)
    out_term = jnp.dot(
        attended.reshape(req_here * token_count, query_cols),
        w_out,
        preferred_element_type=jnp.float32,
    ).reshape(req_here, token_count, -1)
    col_count = out_term.shape[2] // tp_count
    pieces = out_term.reshape(req_here * token_count, tp_count, col_count).transpose(1, 0, 2)
    gathered = lax.all_to_all(pieces, "tp", split_axis=0, concat_axis=0, tiled=True)
    hidden = jnp.sum(gathered, axis=0).astype(jnp.bfloat16).reshape(req_here, token_count, col_count)

    new_cache = rebuild(
        kv_cache, frame_store, incoming, flat_old, flat_new, lengths, keyval, seq_index, token_count
    )
    return (hidden, new_cache)


def solution(mesh):
    placed = (
        P("seq", None, None),
        P(None, "tp"),
        P(),
        P("tp", None),
        P("seq", "tp", None, None),
        P(),
        P(),
        P(),
    )
    return jax.shard_map(
        local,
        mesh=mesh,
        in_specs=placed,
        out_specs=(P("seq", None, "tp"), P("seq", "tp", None, None)),
        check_vma=False,
    )
```

```python
import jax
import jax.numpy as jnp
from jax import lax
from jax.sharding import PartitionSpec as P
from jax.experimental import pallas as pl
from jax.experimental.pallas import tpu as pltpu

WINDOW = 2048
LOW_SCORE = -1e30
HIGH = lax.Precision.HIGH


FRAMES_PER_STEP = 16


def frame_kernel(store_ref, q_ref, mask_ref, out_ref):
    head_dim = q_ref.shape[2] // 2
    page = store_ref[...]
    scores = jnp.einsum(
        "bqc,bkc->bqk", q_ref[...], page, preferred_element_type=jnp.float32
    ) * head_dim ** (-0.5)
    visible = mask_ref[...] > 0
    scores = jnp.where(visible, scores, LOW_SCORE)
    peak = jnp.max(scores, axis=2, keepdims=True)
    weights = jnp.where(visible, jnp.exp(scores - peak), 0.0).astype(jnp.bfloat16)
    total = jnp.sum(weights.astype(jnp.float32), axis=2, keepdims=True)
    mixed = jnp.einsum("bqk,bkc->bqc", weights, page, preferred_element_type=jnp.float32)
    lane = lax.broadcasted_iota(jnp.int32, mixed.shape, 2)
    out_ref[...] = jnp.where(lane == 0, peak, jnp.where(lane == 1, total, mixed))


def frame_attention(store, padded_q, mask):
    frame_total, slot_count, row_width = store.shape
    rows = padded_q.shape[1]
    head_dim = row_width // 2
    step = FRAMES_PER_STEP if frame_total % FRAMES_PER_STEP == 0 else 1
    packed = pl.pallas_call(
        frame_kernel,
        grid=(frame_total // step,),
        in_specs=[
            pl.BlockSpec((step, slot_count, row_width), lambda i: (i, 0, 0)),
            pl.BlockSpec((step, rows, row_width), lambda i: (i, 0, 0)),
            pl.BlockSpec((step, rows, slot_count), lambda i: (i, 0, 0)),
        ],
        out_specs=pl.BlockSpec((step, rows, row_width), lambda i: (i, 0, 0)),
        out_shape=jax.ShapeDtypeStruct((frame_total, rows, row_width), jnp.float32),
        cost_estimate=pl.CostEstimate(
            flops=4 * frame_total * rows * slot_count * row_width,
            transcendentals=frame_total * rows * slot_count,
            bytes_accessed=store.size * 2 + frame_total * rows * (row_width * 6 + 8),
        ),
    )(store, padded_q, mask)
    return packed[..., 0], packed[..., 1], packed[..., head_dim:]


def page_blocks(store, page_frame, lengths, queries, seq_index):
    frame_total, slot_count, row_width = store.shape
    head_dim = row_width // 2
    req_total, token_count, heads_here, _ = queries.shape
    page_count = page_frame.shape[1]
    flat = page_frame.reshape(-1)
    page_ids = jnp.arange(flat.shape[0], dtype=jnp.int32)
    here = seq_index * frame_total + jnp.arange(frame_total, dtype=jnp.int32)
    matches = flat[None, :] == here[:, None]
    owner = jnp.sum(jnp.where(matches, page_ids[None, :], 0), axis=1)
    occupied = jnp.any(matches, axis=1)
    request = owner // page_count
    page_no = owner % page_count
    length = lengths[request]
    rows_per_frame = token_count * heads_here
    padded = jnp.pad(
        queries.reshape(req_total, rows_per_frame, head_dim), ((0, 0), (0, 0), (0, row_width - head_dim))
    )
    frame_q = padded[request]
    token_ids = jnp.arange(token_count, dtype=jnp.int32)
    slot_pos = page_no[:, None] * slot_count + jnp.arange(slot_count, dtype=jnp.int32)[None, :]
    visible = (
        occupied[:, None, None]
        & (slot_pos[:, None, :] < length[:, None, None])
        & (slot_pos[:, None, :] >= (length[:, None] + token_ids[None, :] - WINDOW + 1)[:, :, None])
    )
    mask = jnp.repeat(visible, heads_here, axis=1).astype(jnp.bfloat16)
    peak, total, partial = frame_attention(store, frame_q, mask)
    peak = peak.reshape(frame_total, token_count, heads_here)
    total = total.reshape(frame_total, token_count, heads_here)
    partial = partial.reshape(frame_total, token_count, heads_here, head_dim)
    onehot = request[None, :] == jnp.arange(req_total, dtype=jnp.int32)[:, None]
    local_peak = jnp.max(jnp.where(onehot[:, :, None, None], peak[None], LOW_SCORE), axis=1)
    scale = jnp.exp(peak - local_peak[request])
    onehot_f = onehot.astype(jnp.float32)
    local_total = jnp.einsum("rf,fth->rth", onehot_f, scale * total, precision=HIGH)
    local_partial = jnp.einsum("rf,fthd->rthd", onehot_f, scale[..., None] * partial, precision=HIGH)
    return jnp.concatenate(
        [local_peak[..., None], local_total[..., None], local_partial], axis=-1
    )


def outgoing_pages(frame_store, flat_old, flat_new, seq_index, seq_count):
    frame_total = frame_store.shape[0]
    old_device = flat_old // frame_total
    old_local = flat_old % frame_total
    new_device = flat_new // frame_total
    moving = flat_old != flat_new
    peer_ids = jnp.arange(seq_count, dtype=jnp.int32)[:, None]
    leaving = (
        moving[None, :] & (old_device == seq_index)[None, :] & (new_device[None, :] == peer_ids)
    )
    send_local = jnp.sum(jnp.where(leaving, old_local[None, :], 0), axis=1)
    send_any = jnp.any(leaving, axis=1)
    return jnp.where(
        send_any[:, None, None], frame_store[send_local], jnp.zeros_like(frame_store[send_local])
    )


def rebuild(kv_cache, frame_store, incoming, flat_old, flat_new, lengths, keyval, seq_index, token_count):
    frame_total, slot_count, _ = frame_store.shape
    page_count = flat_new.shape[0] // lengths.shape[0]
    page_ids = jnp.arange(flat_new.shape[0], dtype=jnp.int32)
    here = seq_index * frame_total + jnp.arange(frame_total, dtype=jnp.int32)
    matches = flat_new[None, :] == here[:, None]
    owner = jnp.sum(jnp.where(matches, page_ids[None, :], 0), axis=1)
    occupied = jnp.any(matches, axis=1)
    request = owner // page_count
    page_no = owner % page_count
    token_at = (
        page_no[:, None] * slot_count
        + jnp.arange(slot_count, dtype=jnp.int32)[None, :]
        - lengths[request][:, None]
    )
    fresh = occupied[:, None] & (token_at >= 0) & (token_at < token_count)
    rows_new = keyval[request]
    pick = (token_at[..., None] == jnp.arange(token_count, dtype=jnp.int32)).astype(jnp.bfloat16)
    value = jnp.einsum(
        "fjt,ftc->fjc", pick, rows_new, preferred_element_type=jnp.float32
    ).astype(jnp.bfloat16)
    came_from = flat_old[owner]
    arrived = occupied & (came_from != here)
    source = came_from // frame_total
    moved = jnp.where(arrived[:, None, None, None], incoming[source][:, None], kv_cache)
    return jnp.where(fresh[:, None, :, None], value[:, None], moved)


def local(tokens, w_query, w_keyval, w_out, kv_cache, lengths, page_frame, dest_frame):
    seq_index = lax.axis_index("seq")
    seq_count = lax.axis_size("seq")
    tp_index = lax.axis_index("tp")
    tp_count = lax.axis_size("tp")
    req_here, token_count, model_width = tokens.shape
    req_total = req_here * seq_count
    head_dim = kv_cache.shape[3] // 2
    kv_heads = w_keyval.shape[1] // (2 * head_dim)
    query_cols = w_query.shape[1]
    heads_here = query_cols // head_dim
    kv_group = tp_index // (tp_count // kv_heads)
    kv_columns = lax.dynamic_slice_in_dim(w_keyval, kv_group * 2 * head_dim, 2 * head_dim, 1)
    rows = tokens.reshape(-1, model_width)
    query_here = jnp.dot(rows, w_query, preferred_element_type=jnp.float32).astype(jnp.bfloat16)
    keyval_here = jnp.dot(rows, kv_columns, preferred_element_type=jnp.float32).astype(jnp.bfloat16)
    joined = jnp.concatenate([query_here, keyval_here], axis=1).reshape(
        req_here, token_count, query_cols + 2 * head_dim
    )
    frame_store = kv_cache[:, 0]
    frame_total, slot_count, row_width = frame_store.shape
    flat_old = page_frame.reshape(-1)
    flat_new = dest_frame.reshape(-1)
    outgoing = outgoing_pages(frame_store, flat_old, flat_new, seq_index, seq_count)
    own_size = req_here * token_count * (query_cols + 2 * head_dim)
    own_rows = -(-own_size // row_width)
    own_rows = -(-own_rows // 16) * 16
    own_flat = jnp.pad(joined.reshape(own_size), (0, own_rows * row_width - own_size))
    send = jnp.concatenate(
        [
            outgoing,
            jnp.broadcast_to(own_flat.reshape(1, own_rows, row_width), (seq_count, own_rows, row_width)),
        ],
        axis=1,
    )
    received = lax.all_to_all(send, "seq", split_axis=0, concat_axis=0, tiled=True)
    incoming = received[:, :slot_count]
    joined_all = received[:, slot_count:].reshape(seq_count, own_rows * row_width)[:, :own_size].reshape(
        req_total, token_count, query_cols + 2 * head_dim
    )
    queries = joined_all[..., :query_cols].reshape(req_total, token_count, heads_here, head_dim)
    keyval = joined_all[..., query_cols:]

    blocks = page_blocks(frame_store, page_frame, lengths, queries, seq_index)
    arrived = lax.all_to_all(blocks, "seq", split_axis=0, concat_axis=0, tiled=True)
    arrived = arrived.reshape(seq_count, req_here, token_count, heads_here, head_dim + 2)
    src_peak = arrived[..., 0]
    src_total = arrived[..., 1]
    src_partial = arrived[..., 2:]

    own_q = query_here.reshape(req_here, token_count, heads_here, head_dim)
    own_kv = keyval_here.reshape(req_here, token_count, 2 * head_dim)
    token_ids = jnp.arange(token_count, dtype=jnp.int32)
    causal = (token_ids[:, None] >= token_ids[None, :])[None, :, None, :]
    new_scores = jnp.einsum(
        "rtqd,rud->rtqu", own_q, own_kv[..., :head_dim], preferred_element_type=jnp.float32
    ) * head_dim ** (-0.5)
    new_scores = jnp.where(causal, new_scores, LOW_SCORE)
    new_peak = jnp.max(new_scores, axis=-1)
    new_weights = jnp.where(causal, jnp.exp(new_scores - new_peak[..., None]), 0.0).astype(
        jnp.bfloat16
    )
    new_total = jnp.sum(new_weights.astype(jnp.float32), axis=-1)
    new_partial = jnp.einsum(
        "rtqu,rud->rtqd", new_weights, own_kv[..., head_dim:], preferred_element_type=jnp.float32
    )
    top = jnp.maximum(jnp.max(src_peak, axis=0), new_peak)
    src_scale = jnp.exp(src_peak - top[None])
    new_scale = jnp.exp(new_peak - top)
    denominator = jnp.sum(src_scale * src_total, axis=0) + new_scale * new_total
    numerator = jnp.sum(src_scale[..., None] * src_partial, axis=0) + new_scale[..., None] * new_partial
    attended = (numerator / denominator[..., None]).astype(jnp.bfloat16)
    out_term = jnp.dot(
        attended.reshape(req_here * token_count, query_cols),
        w_out,
        preferred_element_type=jnp.float32,
    ).reshape(req_here, token_count, -1)
    col_count = out_term.shape[2] // tp_count
    pieces = out_term.reshape(req_here * token_count, tp_count, col_count).transpose(1, 0, 2)
    gathered = lax.all_to_all(pieces, "tp", split_axis=0, concat_axis=0, tiled=True)
    hidden = jnp.sum(gathered, axis=0).astype(jnp.bfloat16).reshape(req_here, token_count, col_count)

    new_cache = rebuild(
        kv_cache, frame_store, incoming, flat_old, flat_new, lengths, keyval, seq_index, token_count
    )
    return (hidden, new_cache)


def solution(mesh):
    placed = (
        P("seq", None, None),
        P(None, "tp"),
        P(),
        P("tp", None),
        P("seq", "tp", None, None),
        P(),
        P(),
        P(),
    )
    return jax.shard_map(
        local,
        mesh=mesh,
        in_specs=placed,
        out_specs=(P("seq", None, "tp"), P("seq", "tp", None, None)),
        check_vma=False,
    )
```
